32 devices in a mesh: dp: 4 (over y, core), row: 2 (over x), col: 4 (over z).
Axes of the slice: x: 2, y: 2, z: 4, core: 2. Of those that a mesh axis runs over, the one named last changes fastest.
Arguments:
- block_in: bfloat16 [8192, 1536], P(('dp', 'row', 'col')), may hold values from -6 to 6
- out_grad: bfloat16 [8192, 1536], P(('dp', 'row', 'col')), may hold values from -6 to 6
- norm_gain: float32 [1536], replicated, may hold values from 0.5 to 1.5
- first_norm_gain: float32 [1536], replicated, may hold values from -28 to 28
- second_norm_gain: float32 [1536], replicated, may hold values from 16.384 to 163.84
- input_proj: float32 [1536, 6144], P('dp', ('row', 'col')), may hold values from -0.18371173 to 0.18371173
- first_input_proj: float32 [1536, 6144], P('dp', ('row', 'col')), may hold values from -28 to 28
- second_input_proj: float32 [1536, 6144], P('dp', ('row', 'col')), may hold values from 16.384 to 163.84
- state_proj: float32 [1536, 256], P(('dp', 'row', 'col')), may hold values from -0.15625 to 0.15625
- first_state_proj: float32 [1536, 256], P(('dp', 'row', 'col')), may hold values from -28 to 28
- second_state_proj: float32 [1536, 256], P(('dp', 'row', 'col')), may hold values from 16.384 to 163.84
- step_proj: float32 [1536, 48], P(('dp', 'row', 'col')), may hold values from -0.15625 to 0.15625
- first_step_proj: float32 [1536, 48], P(('dp', 'row', 'col')), may hold values from -28 to 28
- second_step_proj: float32 [1536, 48], P(('dp', 'row', 'col')), may hold values from 16.384 to 163.84
- conv_taps: float32 [5, 3328], replicated, may hold values from -0.5 to 0.5
- first_conv_taps: float32 [5, 3328], replicated, may hold values from -28 to 28
- second_conv_taps: float32 [5, 3328], replicated, may hold values from 16.384 to 163.84
- head_coef: float32 [3, 48], replicated, may hold values from -7 to 3
- first_head_coef: float32 [3, 48], replicated, may hold values from -28 to 28
- second_head_coef: float32 [3, 48], replicated, may hold values from 16.384 to 163.84
- gated_gain: float32 [3072], replicated, may hold values from 0.5 to 1.5
- first_gated_gain: float32 [3072], replicated, may hold values from -28 to 28
- second_gated_gain: float32 [3072], replicated, may hold values from 16.384 to 163.84
- output_proj: float32 [3072, 1536], P(('row', 'col'), 'dp'), may hold values from -0.109375 to 0.109375
- first_output_proj: float32 [3072, 1536], P(('row', 'col'), 'dp'), may hold values from -28 to 28
- second_output_proj: float32 [3072, 1536], P(('row', 'col'), 'dp'), may hold values from 16.384 to 163.84
Outputs:
- block_out: bfloat16 [8192, 1536], P(('dp', 'row', 'col'))
- input_grad: float32 [8192, 1536], P(('dp', 'row', 'col'))
- grad_norm_gain: float32 [1536], replicated
- grad_input_proj: float32 [1536, 6144], P('dp', ('row', 'col'))
- grad_state_proj: float32 [1536, 256], P(('dp', 'row', 'col'))
- grad_step_proj: float32 [1536, 48], P(('dp', 'row', 'col'))
- grad_conv_taps: float32 [5, 3328], replicated
- grad_head_coef: float32 [3, 48], replicated
- grad_gated_gain: float32 [3072], replicated
- grad_output_proj: float32 [3072, 1536], P(('row', 'col'), 'dp')
- new_norm_gain: float32 [1536], replicated
- new_first_norm_gain: float32 [1536], replicated
- new_second_norm_gain: float32 [1536], replicated
- new_input_proj: float32 [1536, 6144], P('dp', ('row', 'col'))
- new_first_input_proj: float32 [1536, 6144], P('dp', ('row', 'col'))
- new_second_input_proj: float32 [1536, 6144], P('dp', ('row', 'col'))
- new_state_proj: float32 [1536, 256], P(('dp', 'row', 'col'))
- new_first_state_proj: float32 [1536, 256], P(('dp', 'row', 'col'))
- new_second_state_proj: float32 [1536, 256], P(('dp', 'row', 'col'))
- new_step_proj: float32 [1536, 48], P(('dp', 'row', 'col'))
- new_first_step_proj: float32 [1536, 48], P(('dp', 'row', 'col'))
- new_second_step_proj: float32 [1536, 48], P(('dp', 'row', 'col'))
- new_conv_taps: float32 [5, 3328], replicated
- new_first_conv_taps: float32 [5, 3328], replicated
- new_second_conv_taps: float32 [5, 3328], replicated
- new_head_coef: float32 [3, 48], replicated
- new_first_head_coef: float32 [3, 48], replicated
- new_second_head_coef: float32 [3, 48], replicated
- new_gated_gain: float32 [3072], replicated
- new_first_gated_gain: float32 [3072], replicated
- new_second_gated_gain: float32 [3072], replicated
- new_output_proj: float32 [3072, 1536], P(('row', 'col'), 'dp')
- new_first_output_proj: float32 [3072, 1536], P(('row', 'col'), 'dp')
- new_second_output_proj: float32 [3072, 1536], P(('row', 'col'), 'dp')
The draws below stay inside these ranges and needn't reach their ends.
All inputs are finite; a program needn't handle non-finite values.
Results may differ from the reference program's by a relative error of at most 0.0034.
The reference program's roundings to bfloat16 on the way count: a program that leaves them out, or rounds other values in their place, can miss the bound.
Values may be sent and summed in bfloat16 or wider, within the bound.
No kernel may reach another device: no remote copies, remote signals or barrier semaphores. Data moves between devices by JAX's collectives and lax.ppermute only.
A program may use at most 192 MiB of HBM per device.

```python
import math
import jax
import jax.numpy as jnp
from jax import lax

D = 1536
NH = 48
HEADDIM = 64
N = 128
SPAN = 256
SEQ_LEN = 1024
ADAM_STEP = 4
INNER = 3072
CONV_CH = 3328
TOKENS = 8192


def draw_input_proj(key, part):
    shape = (D, 2 * INNER)
    noise = jnp.clip(jax.random.normal(key, shape, jnp.float32), -4.0, 4.0)
    column = jnp.arange(2 * INNER) // (2 * HEADDIM)
    scale = 0.6 * jnp.exp(math.log(3.0) * column.astype(jnp.float32) / (NH - 1)) / math.sqrt(D)
    return noise * scale[None, :]


def draw_head_coef(key, part):
    key_one, key_two, key_three = jax.random.split(key, 3)
    step_low = jax.random.uniform(key_one, (NH,), jnp.float32, math.log(0.001), math.log(0.1))
    rate_log = jax.random.uniform(key_two, (NH,), jnp.float32, 0.0, math.log(16.0))
    bias = jnp.log(jnp.expm1(jnp.exp(step_low)))
    skip = jax.random.uniform(key_three, (NH,), jnp.float32, 0.5, 1.5)
    return jnp.stack([bias, rate_log, skip])


def shard_levels(rng, shape, shards, smallest, top_value):
    def one(position, parts):
        steps = jax.random.uniform(jax.random.fold_in(jax.random.fold_in(rng, 6), position), (parts,), jnp.float32, smallest / len(shards), top_value / len(shards))
        return jnp.repeat(jnp.exp(steps), shape[position] // parts).reshape((-1,) + (1,) * (len(shape) - position - 1))

    level = one(*shards[0])
    for cut in shards[1:]:
        level = level * one(*cut)
    return level


def centred(rng, extent, scale, bound, cuts=(), held_as=jnp.bfloat16):
    values = scale * jax.random.normal(rng, extent, jnp.float32)
    if cuts:
        values = values * shard_levels(rng, extent, cuts, -0.22, 0.18)
    return jnp.clip(values, -bound, bound).astype(held_as)


def setup_inputs(seed: int = 0) -> dict:
    key_of = jax.random.split(jax.random.key(seed), 27)
    block_in = centred(key_of[0], (TOKENS, D), 1.0, 6.0, ((0, 32),))
    out_grad = centred(key_of[1], (TOKENS, D), 1.0, 6.0, ((0, 32),))
    norm_gain = jnp.clip(1.0 + 0.1 * jax.random.normal(key_of[2], (D,), jnp.float32), 0.5, 1.5)
    first_norm_gain = centred(key_of[3], (D,), (0.05 * TOKENS ** 0.5), 28.0, (), jnp.float32)
    second_norm_gain = jnp.clip(jnp.exp(jax.random.uniform(key_of[4], (D,), jnp.float32, math.log(16.384), math.log(163.84))), 16.384, 163.84)
    input_proj = draw_input_proj(jax.random.fold_in(key_of[26], 71), 0)
    first_input_proj = centred(key_of[6], (D, 2 * INNER), (0.05 * TOKENS ** 0.5), 28.0, ((0, 4), (1, 8)), jnp.float32)
    second_input_proj = jnp.clip(jnp.exp(math.log(163.84) - 2.30258502 * jax.random.uniform(key_of[7], (D, 2 * INNER), jnp.float32) ** shard_levels(key_of[7], (D, 2 * INNER), ((0, 4), (1, 8)), -0.2, 0.2)), 16.384, 163.84)
    state_proj = centred(key_of[8], (D, 2 * N), D ** -0.5, 0.15625, ((0, 32),), jnp.float32)
    first_state_proj = centred(key_of[9], (D, 2 * N), (0.05 * TOKENS ** 0.5), 28.0, ((0, 32),), jnp.float32)
    second_state_proj = jnp.clip(jnp.exp(math.log(163.84) - 2.30258502 * jax.random.uniform(key_of[10], (D, 2 * N), jnp.float32) ** shard_levels(key_of[10], (D, 2 * N), ((0, 32),), -0.2, 0.2)), 16.384, 163.84)
    step_proj = centred(key_of[11], (D, NH), D ** -0.5, 0.15625, ((0, 32),), jnp.float32)
    first_step_proj = centred(key_of[12], (D, NH), (0.05 * TOKENS ** 0.5), 28.0, ((0, 32),), jnp.float32)
    second_step_proj = jnp.clip(jnp.exp(math.log(163.84) - 2.30258502 * jax.random.uniform(key_of[13], (D, NH), jnp.float32) ** shard_levels(key_of[13], (D, NH), ((0, 32),), -0.2, 0.2)), 16.384, 163.84)
    conv_taps = jnp.clip(jax.random.uniform(key_of[14], (5, CONV_CH), jnp.float32, -0.5, 0.5), -0.5, 0.5)
    first_conv_taps = centred(key_of[15], (5, CONV_CH), (0.05 * TOKENS ** 0.5), 28.0, (), jnp.float32)
    second_conv_taps = jnp.clip(jnp.exp(jax.random.uniform(key_of[16], (5, CONV_CH), jnp.float32, math.log(16.384), math.log(163.84))), 16.384, 163.84)
    head_coef = draw_head_coef(jax.random.fold_in(key_of[26], 71), 0)
    first_head_coef = centred(key_of[18], (3, NH), (0.05 * TOKENS ** 0.5), 28.0, (), jnp.float32)
    second_head_coef = jnp.clip(jnp.exp(jax.random.uniform(key_of[19], (3, NH), jnp.float32, math.log(16.384), math.log(163.84))), 16.384, 163.84)
    gated_gain = jnp.clip(1.0 + 0.1 * jax.random.normal(key_of[20], (INNER,), jnp.float32), 0.5, 1.5)
    first_gated_gain = centred(key_of[21], (INNER,), (0.05 * TOKENS ** 0.5), 28.0, (), jnp.float32)
    second_gated_gain = jnp.clip(jnp.exp(jax.random.uniform(key_of[22], (INNER,), jnp.float32, math.log(16.384), math.log(163.84))), 16.384, 163.84)
    output_proj = centred(key_of[23], (INNER, D), INNER ** -0.5, 0.109375, ((0, 8), (1, 4)), jnp.float32)
    first_output_proj = centred(key_of[24], (INNER, D), (0.05 * TOKENS ** 0.5), 28.0, ((0, 8), (1, 4)), jnp.float32)
    second_output_proj = jnp.clip(jnp.exp(math.log(163.84) - 2.30258502 * jax.random.uniform(key_of[25], (INNER, D), jnp.float32) ** shard_levels(key_of[25], (INNER, D), ((0, 8), (1, 4)), -0.2, 0.2)), 16.384, 163.84)
    return {"block_in": block_in, "out_grad": out_grad, "norm_gain": norm_gain, "first_norm_gain": first_norm_gain, "second_norm_gain": second_norm_gain, "input_proj": input_proj, "first_input_proj": first_input_proj, "second_input_proj": second_input_proj, "state_proj": state_proj, "first_state_proj": first_state_proj, "second_state_proj": second_state_proj, "step_proj": step_proj, "first_step_proj": first_step_proj, "second_step_proj": second_step_proj, "conv_taps": conv_taps, "first_conv_taps": first_conv_taps, "second_conv_taps": second_conv_taps, "head_coef": head_coef, "first_head_coef": first_head_coef, "second_head_coef": second_head_coef, "gated_gain": gated_gain, "first_gated_gain": first_gated_gain, "second_gated_gain": second_gated_gain, "output_proj": output_proj, "first_output_proj": first_output_proj, "second_output_proj": second_output_proj}


PRECISE = lax.Precision.HIGHEST
NORM_EPS = 1e-05
BETA_ONE = 0.9
BETA_TWO = 0.95
ADAM_EPS = 1e-08
MATRIX_RATE = 0.003
VECTOR_RATE = 0.1
WEIGHT_DECAY = 0.1

@jax.custom_vjp
def low(v):
    return lax.optimization_barrier(v.astype(jnp.bfloat16)).astype(jnp.float32)

@jax.custom_vjp
def low_back(v):
    return v

def low_keep(v):
    return (low(v), None)

def low_pass(kept, grad):
    return (grad,)

def back_keep(v):
    return (v, None)

def back_low(kept, grad):
    return (low(grad),)
low.defvjp(low_keep, low_pass)
low_back.defvjp(back_keep, back_low)

def causal_conv(values, filters):
    length = values.shape[0]
    padded = jnp.pad(values, ((3, 0), (0, 0)))
    summed = filters[4][None, :] + jnp.zeros_like(values)
    for offset in range(4):
        summed = summed + filters[offset][None, :] * padded[offset:offset + length]
    return summed

def span_scan(values, deltas, rates, key_rows, query_rows):
    length, head_count, head_width = values.shape
    states = key_rows.shape[1]
    blocks = length // SPAN
    values = values.reshape(blocks, SPAN, head_count, head_width)
    deltas = deltas.reshape(blocks, SPAN, head_count)
    key_rows = key_rows.reshape(blocks, SPAN, states)
    query_rows = query_rows.reshape(blocks, SPAN, states)
    log_decay = jnp.cumsum(deltas * rates[None, None, :], axis=1)
    scores = jnp.einsum('kqn,krn->kqr', query_rows, key_rows, precision=PRECISE)
    causal = jnp.arange(SPAN)[:, None] >= jnp.arange(SPAN)[None, :]
    spread = log_decay[:, :, None, :] - log_decay[:, None, :, :]
    decays = jnp.exp(jnp.where(causal[None, :, :, None], spread, -jnp.inf))
    mixing = scores[:, :, :, None] * decays * deltas[:, None, :, :]
    within = jnp.einsum('kqrh,krhp->kqhp', mixing, values, precision=PRECISE)
    to_end = jnp.exp(log_decay[:, -1:, :] - log_decay) * deltas
    produced = jnp.einsum('kqn,kqh,kqhp->khnp', key_rows, to_end, values, precision=PRECISE)
    factors = jnp.exp(log_decay[:, -1, :])
    carried = jnp.zeros((head_count, states, head_width), jnp.float32)
    entering = []
    for number in range(blocks):
        entering.append(carried)
        carried = carried * factors[number][:, None, None] + produced[number]
    entering = jnp.stack(entering)
    across = jnp.einsum('kqn,khnp->kqhp', query_rows, entering, precision=PRECISE) * jnp.exp(log_decay)[:, :, :, None]
    return (within + across).reshape(length, head_count, head_width)

def mixer_sequence(gate_part, inputs, state_in, step_raw, conv_inner, conv_state, coefs):
    length = inputs.shape[0]
    head_count = coefs.shape[1]
    head_width = inputs.shape[1] // head_count
    state_size = state_in.shape[1] // 2
    conv_out = jax.nn.silu(causal_conv(inputs, conv_inner))
    state_out = jax.nn.silu(causal_conv(state_in, conv_state))
    deltas = jax.nn.softplus(step_raw + coefs[0][None, :])
    rates = -jnp.exp(coefs[1])
    shaped = conv_out.reshape(length, head_count, head_width)
    result = span_scan(shaped, deltas, rates, state_out[:, :state_size], state_out[:, state_size:])
    result = result + coefs[2][None, :, None] * shaped
    return result.reshape(length, head_count * head_width) * jax.nn.silu(gate_part)

def forward(x_float, norm_gain, input_proj, state_proj, step_proj, conv_taps, head_coef, gated_gain, output_proj):
    inv_rms = lax.rsqrt(lax.optimization_barrier(jnp.mean(x_float * x_float, axis=1, keepdims=True)) + NORM_EPS)
    normed_in = low(x_float * inv_rms * norm_gain[None, :])
    projected = low_back(jnp.dot(normed_in, low(input_proj), precision=PRECISE))
    state_in = low_back(low(jnp.dot(normed_in, low(state_proj), precision=PRECISE)))
    step_raw = low_back(low(jnp.dot(normed_in, low(step_proj), precision=PRECISE)))
    paired = projected.reshape(TOKENS, NH, 2, HEADDIM)
    gate_part = paired[:, :, 0, :].reshape(TOKENS, INNER)
    inputs = paired[:, :, 1, :].reshape(TOKENS, INNER)
    conv_inner = conv_taps[:, :INNER]
    conv_state = conv_taps[:, INNER:]
    seq_count = TOKENS // SEQ_LEN

    def sequence(pieces):
        return mixer_sequence(pieces[0], pieces[1], pieces[2], pieces[3], conv_inner, conv_state, head_coef)
    gated = lax.map(jax.checkpoint(sequence), (gate_part.reshape(seq_count, SEQ_LEN, INNER), inputs.reshape(seq_count, SEQ_LEN, INNER), state_in.reshape(seq_count, SEQ_LEN, 2 * N), step_raw.reshape(seq_count, SEQ_LEN, NH)))
    gated = gated.reshape(TOKENS, INNER)
    gated_rms = lax.rsqrt(lax.optimization_barrier(jnp.mean(gated * gated, axis=1, keepdims=True)) + NORM_EPS)
    normed_out = low(gated * gated_rms * gated_gain[None, :])
    return x_float + jnp.dot(normed_out, low(output_proj), precision=PRECISE)

def adamw(weight, gradient, moment_one, moment_two, step_rate, shrink):
    new_one = BETA_ONE * moment_one + (1.0 - BETA_ONE) * gradient
    new_two = BETA_TWO * moment_two + (1.0 - BETA_TWO) * gradient * gradient
    one_hat = new_one / (1.0 - BETA_ONE ** ADAM_STEP)
    two_hat = new_two / (1.0 - BETA_TWO ** ADAM_STEP)
    updated = weight - step_rate * (one_hat / (jnp.sqrt(two_hat) + ADAM_EPS) + shrink * weight)
    return (updated, new_one, new_two)

def reference(block_in, out_grad, norm_gain, first_norm_gain, second_norm_gain, input_proj, first_input_proj, second_input_proj, state_proj, first_state_proj, second_state_proj, step_proj, first_step_proj, second_step_proj, conv_taps, first_conv_taps, second_conv_taps, head_coef, first_head_coef, second_head_coef, gated_gain, first_gated_gain, second_gated_gain, output_proj, first_output_proj, second_output_proj):
    result, pull = jax.vjp(forward, block_in.astype(jnp.float32), norm_gain, input_proj, state_proj, step_proj, conv_taps, head_coef, gated_gain, output_proj)
    grads = pull(out_grad.astype(jnp.float32))
    block_out = result.astype(jnp.bfloat16)
    input_grad = grads[0]
    g_norm, g_input, g_state, g_step, g_conv, g_head, g_gated, g_output = (grads[1], grads[2], grads[3], grads[4], grads[5], grads[6], grads[7], grads[8])
    n_norm, f_norm, s_norm = adamw(norm_gain, g_norm, first_norm_gain, second_norm_gain, VECTOR_RATE, 0.0)
    n_input, f_input, s_input = adamw(input_proj, g_input, first_input_proj, second_input_proj, MATRIX_RATE, WEIGHT_DECAY)
    n_state, f_state, s_state = adamw(state_proj, g_state, first_state_proj, second_state_proj, MATRIX_RATE, WEIGHT_DECAY)
    n_step, f_step, s_step = adamw(step_proj, g_step, first_step_proj, second_step_proj, MATRIX_RATE, WEIGHT_DECAY)
    n_conv, f_conv, s_conv = adamw(conv_taps, g_conv, first_conv_taps, second_conv_taps, VECTOR_RATE, 0.0)
    n_head, f_head, s_head = adamw(head_coef, g_head, first_head_coef, second_head_coef, VECTOR_RATE, 0.0)
    n_gated, f_gated, s_gated = adamw(gated_gain, g_gated, first_gated_gain, second_gated_gain, VECTOR_RATE, 0.0)
    n_output, f_output, s_output = adamw(output_proj, g_output, first_output_proj, second_output_proj, MATRIX_RATE, WEIGHT_DECAY)
    return (block_out, input_grad, g_norm, g_input, g_state, g_step, g_conv, g_head, g_gated, g_output, n_norm, f_norm, s_norm, n_input, f_input, s_input, n_state, f_state, s_state, n_step, f_step, s_step, n_conv, f_conv, s_conv, n_head, f_head, s_head, n_gated, f_gated, s_gated, n_output, f_output, s_output)
```

```python
import jax
import jax.numpy as jnp
from jax import lax
from jax.sharding import PartitionSpec as P


SPAN = 256
SEQ_LEN = 1024
ADAM_STEP = 4


PRECISE = lax.Precision.HIGHEST
NORM_EPS = 1e-05
BETA_ONE = 0.9
BETA_TWO = 0.95
ADAM_EPS = 1e-08
MATRIX_RATE = 0.003
VECTOR_RATE = 0.1
WEIGHT_DECAY = 0.1


def causal_conv(values, filters):
    length = values.shape[0]
    padded = jnp.pad(values, ((3, 0), (0, 0)))
    summed = filters[4][None, :] + jnp.zeros_like(values)
    for offset in range(4):
        summed = summed + filters[offset][None, :] * padded[offset : offset + length]
    return summed


def span_scan(values, deltas, rates, key_rows, query_rows):
    length, head_count, head_width = values.shape
    states = key_rows.shape[1]
    blocks = length // SPAN
    values = values.reshape(blocks, SPAN, head_count, head_width)
    deltas = deltas.reshape(blocks, SPAN, head_count)
    key_rows = key_rows.reshape(blocks, SPAN, states)
    query_rows = query_rows.reshape(blocks, SPAN, states)
    log_decay = jnp.cumsum(deltas * rates[None, None, :], axis=1)
    scores = jnp.einsum("kqn,krn->kqr", query_rows, key_rows, precision=PRECISE)
    causal = jnp.arange(SPAN)[:, None] >= jnp.arange(SPAN)[None, :]
    head_decay = jnp.transpose(log_decay, (0, 2, 1))
    head_deltas = jnp.transpose(deltas, (0, 2, 1))
    spread = head_decay[:, :, :, None] - head_decay[:, :, None, :]
    decays = jnp.exp(jnp.where(causal[None, None, :, :], spread, -jnp.inf))
    mixing = scores[:, None, :, :] * decays * head_deltas[:, :, None, :]
    within = jnp.einsum("khqr,krhp->kqhp", mixing, values, precision=PRECISE)
    to_end = jnp.exp(log_decay[:, -1:, :] - log_decay) * deltas
    produced = jnp.einsum("kqn,kqh,kqhp->khnp", key_rows, to_end, values, precision=PRECISE)
    factors = jnp.exp(log_decay[:, -1, :])
    carried = jnp.zeros((head_count, states, head_width), jnp.float32)
    entering = []
    for number in range(blocks):
        entering.append(carried)
        carried = carried * factors[number][:, None, None] + produced[number]
    entering = jnp.stack(entering)
    across = (
        jnp.einsum("kqn,khnp->kqhp", query_rows, entering, precision=PRECISE)
        * jnp.exp(log_decay)[:, :, :, None]
    )
    return (within + across).reshape(length, head_count, head_width)


def mixer_sequence(gate_part, inputs, state_in, step_raw, conv_inner, conv_state, coefs):
    length = inputs.shape[0]
    head_count = coefs.shape[1]
    head_width = inputs.shape[1] // head_count
    state_size = state_in.shape[1] // 2
    conv_out = jax.nn.silu(causal_conv(inputs, conv_inner))
    state_out = jax.nn.silu(causal_conv(state_in, conv_state))
    deltas = jax.nn.softplus(step_raw + coefs[0][None, :])
    rates = -jnp.exp(coefs[1])
    shaped = conv_out.reshape(length, head_count, head_width)
    result = span_scan(shaped, deltas, rates, state_out[:, :state_size], state_out[:, state_size:])
    result = result + coefs[2][None, :, None] * shaped
    return result.reshape(length, head_count * head_width) * jax.nn.silu(gate_part)


def mixer_all(gate_part, inputs, state_in, step_raw, conv_inner, conv_state, coefs):
    seq_count = inputs.shape[0] // SEQ_LEN

    def sequence(pieces):
        return mixer_sequence(
            pieces[0], pieces[1], pieces[2], pieces[3], conv_inner, conv_state, coefs
        )

    gated = lax.map(
        jax.checkpoint(sequence),
        (
            gate_part.reshape(seq_count, SEQ_LEN, -1),
            inputs.reshape(seq_count, SEQ_LEN, -1),
            state_in.reshape(seq_count, SEQ_LEN, -1),
            step_raw.reshape(seq_count, SEQ_LEN, -1),
        ),
    )
    return gated.reshape(inputs.shape[0], -1)


def adamw(weight, gradient, moment_one, moment_two, step_rate, shrink):
    new_one = BETA_ONE * moment_one + (1.0 - BETA_ONE) * gradient
    new_two = BETA_TWO * moment_two + (1.0 - BETA_TWO) * gradient * gradient
    one_hat = new_one / (1.0 - BETA_ONE**ADAM_STEP)
    two_hat = new_two / (1.0 - BETA_TWO**ADAM_STEP)
    updated = weight - step_rate * (one_hat / (jnp.sqrt(two_hat) + ADAM_EPS) + shrink * weight)
    return (updated, new_one, new_two)


def pack_rows(values, width):
    flat = values.reshape(-1)
    rows = -(-flat.shape[0] // width)
    return jnp.pad(flat, (0, rows * width - flat.shape[0])).reshape(rows, width)


def per_device(
    block_in,
    out_grad,
    norm_gain,
    first_norm_gain,
    second_norm_gain,
    input_proj,
    first_input_proj,
    second_input_proj,
    state_proj,
    first_state_proj,
    second_state_proj,
    step_proj,
    first_step_proj,
    second_step_proj,
    conv_taps,
    first_conv_taps,
    second_conv_taps,
    head_coef,
    first_head_coef,
    second_head_coef,
    gated_gain,
    first_gated_gain,
    second_gated_gain,
    output_proj,
    first_output_proj,
    second_output_proj,
):
    groups = lax.axis_size(("row", "col"))
    dps = lax.axis_size("dp")
    place = lax.axis_index(("row", "col"))
    tok_dev = block_in.shape[0]
    model = block_in.shape[1]
    group_tok = tok_dev * groups
    inner = gated_gain.shape[0]
    inner_dev = inner // groups
    head_total = head_coef.shape[1]
    heads_dev = head_total // groups
    head_width = inner // head_total
    n_state = state_proj.shape[1]
    n_small = n_state + step_proj.shape[1]
    rows_dev = state_proj.shape[0]
    in_rows, in_cols = input_proj.shape
    small = jnp.concatenate([state_proj, step_proj], axis=1).astype(jnp.bfloat16)
    small_flat = rows_dev * n_small
    stage_one = lax.all_gather(
        jnp.concatenate(
            [input_proj.astype(jnp.bfloat16), pack_rows(small, in_cols)], axis=0
        ),
        "dp",
        axis=0,
    )
    in_local = stage_one[:, :in_rows].reshape(dps * in_rows, in_cols)
    small_dp = stage_one[:, in_rows:].reshape(dps, -1)[:, :small_flat]
    out_local = lax.all_gather(output_proj.astype(jnp.bfloat16), "dp", axis=1, tiled=True)
    x_float = block_in.astype(jnp.float32)
    inv_rms = lax.rsqrt(jnp.mean(x_float * x_float, axis=1, keepdims=True) + NORM_EPS)
    normed_in = (x_float * inv_rms * norm_gain[None, :]).astype(jnp.bfloat16)
    stage_two = lax.all_gather(
        jnp.concatenate([normed_in, pack_rows(small_dp, model)], axis=0),
        ("row", "col"),
        axis=0,
    )
    normed_all = stage_two[:, :tok_dev].reshape(group_tok, model)
    small_full = (
        stage_two[:, tok_dev:]
        .reshape(groups, -1)[:, : dps * small_flat]
        .reshape(groups, dps, rows_dev, n_small)
        .transpose(1, 0, 2, 3)
        .reshape(dps * groups * rows_dev, n_small)
    )
    cotangent = lax.all_gather(out_grad, ("row", "col"), axis=0, tiled=True)
    projected = jnp.dot(normed_all, in_local, preferred_element_type=jnp.float32)
    small_all = jnp.dot(normed_all, small_full, preferred_element_type=jnp.float32).astype(
        jnp.bfloat16
    )
    state_all = small_all[:, :n_state]
    step_all = small_all[:, n_state:]
    paired = projected.reshape(group_tok, heads_dev, 2, head_width)
    gate_part = paired[:, :, 0, :].reshape(group_tok, inner_dev)
    inputs = paired[:, :, 1, :].reshape(group_tok, inner_dev)
    conv_inner = lax.dynamic_slice_in_dim(conv_taps, place * inner_dev, inner_dev, 1)
    conv_state = conv_taps[:, inner:]
    coefs = lax.dynamic_slice_in_dim(head_coef, place * heads_dev, heads_dev, 1)
    step_local = lax.dynamic_slice_in_dim(step_all, place * heads_dev, heads_dev, 1).astype(
        jnp.float32
    )
    gated, mixer_pull = jax.vjp(
        mixer_all,
        gate_part,
        inputs,
        state_all.astype(jnp.float32),
        step_local,
        conv_inner,
        conv_state,
        coefs,
    )
    squares = lax.psum(jnp.sum(gated * gated, axis=1), ("row", "col"))
    gated_rms = lax.rsqrt(squares / inner + NORM_EPS)[:, None]
    gain_local = lax.dynamic_slice_in_dim(gated_gain, place * inner_dev, inner_dev, 0)
    normed_out = (gated * gated_rms * gain_local[None, :]).astype(jnp.bfloat16)
    mixed = lax.psum_scatter(
        jnp.dot(normed_out, out_local, preferred_element_type=jnp.float32),
        ("row", "col"),
        scatter_dimension=0,
        tiled=True,
    )
    block_out = (x_float + mixed).astype(jnp.bfloat16)
    grad_out_local = jnp.einsum(
        "tc,td->cd", normed_out, cotangent, preferred_element_type=jnp.float32
    )
    grad_output = lax.psum_scatter(grad_out_local, "dp", scatter_dimension=1, tiled=True)
    d_normed = jnp.einsum("td,cd->tc", cotangent, out_local, preferred_element_type=jnp.float32)
    gain_part = jnp.sum(d_normed * gated * gated_rms, axis=0)
    scaled = d_normed * gain_local[None, :]
    cross = lax.psum(jnp.sum(scaled * gated, axis=1), ("row", "col"))
    d_gated = gated_rms * scaled - gated * gated_rms**3 * (cross / inner)[:, None]
    d_gate, d_inputs, d_state, d_step, d_conv_inner, d_conv_state, d_coefs = mixer_pull(
        d_gated
    )
    d_projected = (
        jnp.stack(
            [
                d_gate.reshape(group_tok, heads_dev, head_width),
                d_inputs.reshape(group_tok, heads_dev, head_width),
            ],
            axis=2,
        )
        .reshape(group_tok, 2 * inner_dev)
        .astype(jnp.bfloat16)
    )
    grad_in_local = jnp.einsum(
        "td,tc->dc", normed_all, d_projected, preferred_element_type=jnp.float32
    )
    step_spread = lax.dynamic_update_slice_in_dim(
        jnp.zeros((group_tok, head_total), jnp.float32), d_step, place * heads_dev, 1
    )
    back_all = lax.psum_scatter(
        jnp.concatenate(
            [
                jnp.einsum("tc,dc->td", d_projected, in_local, preferred_element_type=jnp.float32),
                d_state,
                step_spread,
            ],
            axis=1,
        ),
        ("row", "col"),
        scatter_dimension=0,
        tiled=True,
    )
    d_normed_in = back_all[:, :model]
    small_back = back_all[:, model:].astype(jnp.bfloat16)
    d_normed_in = d_normed_in + jnp.einsum(
        "tc,dc->td", small_back, small_full, preferred_element_type=jnp.float32
    )
    grad_small_part = jnp.einsum(
        "td,tc->dc", normed_in, small_back, preferred_element_type=jnp.float32
    )
    grad_input = lax.psum_scatter(grad_in_local, "dp", scatter_dimension=0, tiled=True)
    scaled_in = d_normed_in * norm_gain[None, :]
    norm_part = jnp.sum(d_normed_in * x_float * inv_rms, axis=0)
    input_grad = (
        out_grad.astype(jnp.float32)
        + inv_rms * scaled_in
        - x_float * inv_rms**3 * jnp.mean(scaled_in * x_float, axis=1, keepdims=True)
    )
    gated_spread = lax.dynamic_update_slice_in_dim(
        jnp.zeros((inner,), jnp.float32), gain_part, place * inner_dev, 0
    )
    conv_front = lax.dynamic_update_slice_in_dim(
        jnp.zeros((5, inner), jnp.float32), d_conv_inner, place * inner_dev, 1
    )
    conv_spread = jnp.concatenate([conv_front, d_conv_state], axis=1)
    coef_spread = lax.dynamic_update_slice_in_dim(
        jnp.zeros((3, head_total), jnp.float32), d_coefs, place * heads_dev, 1
    )
    pieces = (norm_part, gated_spread, conv_spread, coef_spread, grad_small_part)
    summed = lax.psum(
        jnp.concatenate([piece.reshape(-1) for piece in pieces]), ("dp", "row", "col")
    )
    offsets = [0]
    for piece in pieces:
        offsets.append(offsets[-1] + piece.size)
    grad_norm, grad_gated, grad_conv, grad_coef, grad_small_all = (
        summed[offsets[k] : offsets[k + 1]].reshape(piece.shape)
        for k, piece in enumerate(pieces)
    )
    me = lax.axis_index(("dp", "row", "col"))
    grad_small = lax.dynamic_slice_in_dim(grad_small_all, me * rows_dev, rows_dev, 0)
    grad_state = grad_small[:, :n_state]
    grad_step = grad_small[:, n_state:]
    n_norm, f_norm, s_norm = adamw(
        norm_gain, grad_norm, first_norm_gain, second_norm_gain, VECTOR_RATE, 0.0
    )
    n_input, f_input, s_input = adamw(
        input_proj, grad_input, first_input_proj, second_input_proj, MATRIX_RATE, WEIGHT_DECAY
    )
    n_state, f_state, s_state = adamw(
        state_proj, grad_state, first_state_proj, second_state_proj, MATRIX_RATE, WEIGHT_DECAY
    )
    n_step, f_step, s_step = adamw(
        step_proj, grad_step, first_step_proj, second_step_proj, MATRIX_RATE, WEIGHT_DECAY
    )
    n_conv, f_conv, s_conv = adamw(
        conv_taps, grad_conv, first_conv_taps, second_conv_taps, VECTOR_RATE, 0.0
    )
    n_head, f_head, s_head = adamw(
        head_coef, grad_coef, first_head_coef, second_head_coef, VECTOR_RATE, 0.0
    )
    n_gated, f_gated, s_gated = adamw(
        gated_gain, grad_gated, first_gated_gain, second_gated_gain, VECTOR_RATE, 0.0
    )
    n_output, f_output, s_output = adamw(
        output_proj, grad_output, first_output_proj, second_output_proj, MATRIX_RATE, WEIGHT_DECAY
    )
    return (
        block_out,
        input_grad,
        grad_norm,
        grad_input,
        grad_state,
        grad_step,
        grad_conv,
        grad_coef,
        grad_gated,
        grad_output,
        n_norm,
        f_norm,
        s_norm,
        n_input,
        f_input,
        s_input,
        n_state,
        f_state,
        s_state,
        n_step,
        f_step,
        s_step,
        n_conv,
        f_conv,
        s_conv,
        n_head,
        f_head,
        s_head,
        n_gated,
        f_gated,
        s_gated,
        n_output,
        f_output,
        s_output,
    )


def solution(mesh):
    return jax.shard_map(
        per_device,
        mesh=mesh,
        in_specs=(
            P(("dp", "row", "col"), None),
            P(("dp", "row", "col"), None),
            P(),
            P(),
            P(),
            P("dp", ("row", "col")),
            P("dp", ("row", "col")),
            P("dp", ("row", "col")),
            P(("dp", "row", "col"), None),
            P(("dp", "row", "col"), None),
            P(("dp", "row", "col"), None),
            P(("dp", "row", "col"), None),
            P(("dp", "row", "col"), None),
            P(("dp", "row", "col"), None),
            P(),
            P(),
            P(),
            P(),
            P(),
            P(),
            P(),
            P(),
            P(),
            P(("row", "col"), "dp"),
            P(("row", "col"), "dp"),
            P(("row", "col"), "dp"),
        ),
        out_specs=(
            P(("dp", "row", "col"), None),
            P(("dp", "row", "col"), None),
            P(),
            P("dp", ("row", "col")),
            P(("dp", "row", "col"), None),
            P(("dp", "row", "col"), None),
            P(),
            P(),
            P(),
            P(("row", "col"), "dp"),
            P(),
            P(),
            P(),
            P("dp", ("row", "col")),
            P("dp", ("row", "col")),
            P("dp", ("row", "col")),
            P(("dp", "row", "col"), None),
            P(("dp", "row", "col"), None),
            P(("dp", "row", "col"), None),
            P(("dp", "row", "col"), None),
            P(("dp", "row", "col"), None),
            P(("dp", "row", "col"), None),
            P(),
            P(),
            P(),
            P(),
            P(),
            P(),
            P(),
            P(),
            P(),
            P(("row", "col"), "dp"),
            P(("row", "col"), "dp"),
            P(("row", "col"), "dp"),
        ),
        check_vma=False,
    )
```

```python
import jax
import jax.numpy as jnp
from jax import lax
from jax.sharding import PartitionSpec as P


SPAN = 256
SEQ_LEN = 1024
ADAM_STEP = 4


PRECISE = lax.Precision.HIGHEST
NORM_EPS = 1e-05
BETA_ONE = 0.9
BETA_TWO = 0.95
ADAM_EPS = 1e-08
MATRIX_RATE = 0.003
VECTOR_RATE = 0.1
WEIGHT_DECAY = 0.1


def causal_conv(values, filters):
    length = values.shape[0]
    padded = jnp.pad(values, ((3, 0), (0, 0)))
    summed = filters[4][None, :] + jnp.zeros_like(values)
    for offset in range(4):
        summed = summed + filters[offset][None, :] * padded[offset : offset + length]
    return summed


def span_scan(values, deltas, rates, key_rows, query_rows):
    length, head_count, head_width = values.shape
    states = key_rows.shape[1]
    blocks = length // SPAN
    values = values.reshape(blocks, SPAN, head_count, head_width)
    deltas = deltas.reshape(blocks, SPAN, head_count)
    key_rows = key_rows.reshape(blocks, SPAN, states)
    query_rows = query_rows.reshape(blocks, SPAN, states)
    lower = (jnp.arange(SPAN)[:, None] >= jnp.arange(SPAN)[None, :]).astype(jnp.float32)
    log_decay = jnp.einsum("qr,krh->kqh", lower, deltas * rates[None, None, :], precision=PRECISE)
    scores = jnp.einsum("kqn,krn->kqr", query_rows, key_rows, precision=PRECISE)
    causal = jnp.arange(SPAN)[:, None] >= jnp.arange(SPAN)[None, :]
    head_decay = jnp.transpose(log_decay, (0, 2, 1))
    head_deltas = jnp.transpose(deltas, (0, 2, 1))
    spread = head_decay[:, :, :, None] - head_decay[:, :, None, :]
    decays = jnp.exp(jnp.where(causal[None, None, :, :], spread, -jnp.inf))
    mixing = scores[:, None, :, :] * decays * head_deltas[:, :, None, :]
    within = jnp.einsum("khqr,krhp->kqhp", mixing, values, precision=PRECISE)
    to_end = jnp.exp(log_decay[:, -1:, :] - log_decay) * deltas
    produced = jnp.einsum("kqn,kqh,kqhp->khnp", key_rows, to_end, values, precision=PRECISE)
    factors = jnp.exp(log_decay[:, -1, :])
    carried = jnp.zeros((head_count, states, head_width), jnp.float32)
    entering = []
    for number in range(blocks):
        entering.append(carried)
        carried = carried * factors[number][:, None, None] + produced[number]
    entering = jnp.stack(entering)
    across = (
        jnp.einsum("kqn,khnp->kqhp", query_rows, entering, precision=PRECISE)
        * jnp.exp(log_decay)[:, :, :, None]
    )
    return (within + across).reshape(length, head_count, head_width)


def mixer_sequence(gate_part, inputs, state_in, step_raw, conv_inner, conv_state, coefs):
    length = inputs.shape[0]
    head_count = coefs.shape[1]
    head_width = inputs.shape[1] // head_count
    state_size = state_in.shape[1] // 2
    conv_out = jax.nn.silu(causal_conv(inputs, conv_inner))
    state_out = jax.nn.silu(causal_conv(state_in, conv_state))
    deltas = jax.nn.softplus(step_raw + coefs[0][None, :])
    rates = -jnp.exp(coefs[1])
    shaped = conv_out.reshape(length, head_count, head_width)
    result = span_scan(shaped, deltas, rates, state_out[:, :state_size], state_out[:, state_size:])
    result = result + coefs[2][None, :, None] * shaped
    return result.reshape(length, head_count * head_width) * jax.nn.silu(gate_part)


def mixer_all(gate_part, inputs, state_in, step_raw, conv_inner, conv_state, coefs):
    seq_count = inputs.shape[0] // SEQ_LEN

    def sequence(pieces):
        return mixer_sequence(
            pieces[0], pieces[1], pieces[2], pieces[3], conv_inner, conv_state, coefs
        )

    gated = lax.map(
        jax.checkpoint(sequence),
        (
            gate_part.reshape(seq_count, SEQ_LEN, -1),
            inputs.reshape(seq_count, SEQ_LEN, -1),
            state_in.reshape(seq_count, SEQ_LEN, -1),
            step_raw.reshape(seq_count, SEQ_LEN, -1),
        ),
    )
    return gated.reshape(inputs.shape[0], -1)


def adamw(weight, gradient, moment_one, moment_two, step_rate, shrink):
    new_one = BETA_ONE * moment_one + (1.0 - BETA_ONE) * gradient
    new_two = BETA_TWO * moment_two + (1.0 - BETA_TWO) * gradient * gradient
    one_hat = new_one / (1.0 - BETA_ONE**ADAM_STEP)
    two_hat = new_two / (1.0 - BETA_TWO**ADAM_STEP)
    updated = weight - step_rate * (one_hat / (jnp.sqrt(two_hat) + ADAM_EPS) + shrink * weight)
    return (updated, new_one, new_two)


def pack_rows(values, width):
    flat = values.reshape(-1)
    rows = -(-flat.shape[0] // width)
    return jnp.pad(flat, (0, rows * width - flat.shape[0])).reshape(rows, width)


def per_device(
    block_in,
    out_grad,
    norm_gain,
    first_norm_gain,
    second_norm_gain,
    input_proj,
    first_input_proj,
    second_input_proj,
    state_proj,
    first_state_proj,
    second_state_proj,
    step_proj,
    first_step_proj,
    second_step_proj,
    conv_taps,
    first_conv_taps,
    second_conv_taps,
    head_coef,
    first_head_coef,
    second_head_coef,
    gated_gain,
    first_gated_gain,
    second_gated_gain,
    output_proj,
    first_output_proj,
    second_output_proj,
):
    groups = lax.axis_size(("row", "col"))
    dps = lax.axis_size("dp")
    place = lax.axis_index(("row", "col"))
    tok_dev = block_in.shape[0]
    model = block_in.shape[1]
    group_tok = tok_dev * groups
    inner = gated_gain.shape[0]
    inner_dev = inner // groups
    head_total = head_coef.shape[1]
    heads_dev = head_total // groups
    head_width = inner // head_total
    n_state = state_proj.shape[1]
    n_small = n_state + step_proj.shape[1]
    rows_dev = state_proj.shape[0]
    in_rows, in_cols = input_proj.shape
    small = jnp.concatenate([state_proj, step_proj], axis=1).astype(jnp.bfloat16)
    small_flat = rows_dev * n_small
    stage_one = lax.all_gather(
        jnp.concatenate(
            [input_proj.astype(jnp.bfloat16), pack_rows(small, in_cols)], axis=0
        ),
        "dp",
        axis=0,
    )
    in_local = stage_one[:, :in_rows].reshape(dps * in_rows, in_cols)
    small_dp = stage_one[:, in_rows:].reshape(dps, -1)[:, :small_flat]
    out_local = lax.all_gather(output_proj.astype(jnp.bfloat16), "dp", axis=1, tiled=True)
    x_float = block_in.astype(jnp.float32)
    inv_rms = lax.rsqrt(jnp.mean(x_float * x_float, axis=1, keepdims=True) + NORM_EPS)
    normed_in = (x_float * inv_rms * norm_gain[None, :]).astype(jnp.bfloat16)
    stage_two = lax.all_gather(
        jnp.concatenate([normed_in, pack_rows(small_dp, model)], axis=0),
        ("row", "col"),
        axis=0,
    )
    normed_all = stage_two[:, :tok_dev].reshape(group_tok, model)
    small_full = (
        stage_two[:, tok_dev:]
        .reshape(groups, -1)[:, : dps * small_flat]
        .reshape(groups, dps, rows_dev, n_small)
        .transpose(1, 0, 2, 3)
        .reshape(dps * groups * rows_dev, n_small)
    )
    cotangent = lax.all_gather(out_grad, ("row", "col"), axis=0, tiled=True)
    projected = jnp.dot(normed_all, in_local, preferred_element_type=jnp.float32)
    small_all = jnp.dot(normed_all, small_full, preferred_element_type=jnp.float32).astype(
        jnp.bfloat16
    )
    state_all = small_all[:, :n_state]
    step_all = small_all[:, n_state:]
    paired = projected.reshape(group_tok, heads_dev, 2, head_width)
    gate_part = paired[:, :, 0, :].reshape(group_tok, inner_dev)
    inputs = paired[:, :, 1, :].reshape(group_tok, inner_dev)
    conv_inner = lax.dynamic_slice_in_dim(conv_taps, place * inner_dev, inner_dev, 1)
    conv_state = conv_taps[:, inner:]
    coefs = lax.dynamic_slice_in_dim(head_coef, place * heads_dev, heads_dev, 1)
    step_local = lax.dynamic_slice_in_dim(step_all, place * heads_dev, heads_dev, 1).astype(
        jnp.float32
    )
    gated, mixer_pull = jax.vjp(
        mixer_all,
        gate_part,
        inputs,
        state_all.astype(jnp.float32),
        step_local,
        conv_inner,
        conv_state,
        coefs,
    )
    squares = lax.psum(jnp.sum(gated * gated, axis=1), ("row", "col"))
    gated_rms = lax.rsqrt(squares / inner + NORM_EPS)[:, None]
    gain_local = lax.dynamic_slice_in_dim(gated_gain, place * inner_dev, inner_dev, 0)
    normed_out = (gated * gated_rms * gain_local[None, :]).astype(jnp.bfloat16)
    mixed = lax.psum_scatter(
        jnp.dot(normed_out, out_local, preferred_element_type=jnp.float32),
        ("row", "col"),
        scatter_dimension=0,
        tiled=True,
    )
    block_out = (x_float + mixed).astype(jnp.bfloat16)
    grad_out_local = jnp.einsum(
        "tc,td->cd", normed_out, cotangent, preferred_element_type=jnp.float32
    )
    grad_output = lax.psum_scatter(grad_out_local, "dp", scatter_dimension=1, tiled=True)
    d_normed = jnp.einsum("td,cd->tc", cotangent, out_local, preferred_element_type=jnp.float32)
    gain_part = jnp.sum(d_normed * gated * gated_rms, axis=0)
    scaled = d_normed * gain_local[None, :]
    cross = lax.psum(jnp.sum(scaled * gated, axis=1), ("row", "col"))
    d_gated = gated_rms * scaled - gated * gated_rms**3 * (cross / inner)[:, None]
    d_gate, d_inputs, d_state, d_step, d_conv_inner, d_conv_state, d_coefs = mixer_pull(
        d_gated
    )
    d_projected = (
        jnp.stack(
            [
                d_gate.reshape(group_tok, heads_dev, head_width),
                d_inputs.reshape(group_tok, heads_dev, head_width),
            ],
            axis=2,
        )
        .reshape(group_tok, 2 * inner_dev)
        .astype(jnp.bfloat16)
    )
    grad_in_local = jnp.einsum(
        "td,tc->dc", normed_all, d_projected, preferred_element_type=jnp.float32
    )
    step_spread = lax.dynamic_update_slice_in_dim(
        jnp.zeros((group_tok, head_total), jnp.float32), d_step, place * heads_dev, 1
    )
    back_all = lax.psum_scatter(
        jnp.concatenate(
            [
                jnp.einsum("tc,dc->td", d_projected, in_local, preferred_element_type=jnp.float32),
                d_state,
                step_spread,
            ],
            axis=1,
        ),
        ("row", "col"),
        scatter_dimension=0,
        tiled=True,
    )
    d_normed_in = back_all[:, :model]
    small_back = back_all[:, model:].astype(jnp.bfloat16)
    d_normed_in = d_normed_in + jnp.einsum(
        "tc,dc->td", small_back, small_full, preferred_element_type=jnp.float32
    )
    grad_small_part = jnp.einsum(
        "td,tc->dc", normed_in, small_back, preferred_element_type=jnp.float32
    )
    grad_input = lax.psum_scatter(grad_in_local, "dp", scatter_dimension=0, tiled=True)
    scaled_in = d_normed_in * norm_gain[None, :]
    norm_part = jnp.sum(d_normed_in * x_float * inv_rms, axis=0)
    input_grad = (
        out_grad.astype(jnp.float32)
        + inv_rms * scaled_in
        - x_float * inv_rms**3 * jnp.mean(scaled_in * x_float, axis=1, keepdims=True)
    )
    gated_spread = lax.dynamic_update_slice_in_dim(
        jnp.zeros((inner,), jnp.float32), gain_part, place * inner_dev, 0
    )
    conv_front = lax.dynamic_update_slice_in_dim(
        jnp.zeros((5, inner), jnp.float32), d_conv_inner, place * inner_dev, 1
    )
    conv_spread = jnp.concatenate([conv_front, d_conv_state], axis=1)
    coef_spread = lax.dynamic_update_slice_in_dim(
        jnp.zeros((3, head_total), jnp.float32), d_coefs, place * heads_dev, 1
    )
    pieces = (norm_part, gated_spread, conv_spread, coef_spread)
    offsets = [0]
    for piece in pieces:
        offsets.append(offsets[-1] + piece.size)
    packed = pack_rows(jnp.concatenate([piece.reshape(-1) for piece in pieces]), n_small)
    summed = lax.psum(jnp.concatenate([grad_small_part, packed], axis=0), ("dp", "row", "col"))
    grad_small_all = summed[: grad_small_part.shape[0]]
    summed_flat = summed[grad_small_part.shape[0] :].reshape(-1)
    grad_norm, grad_gated, grad_conv, grad_coef = (
        summed_flat[offsets[k] : offsets[k + 1]].reshape(piece.shape)
        for k, piece in enumerate(pieces)
    )
    me = lax.axis_index(("dp", "row", "col"))
    grad_small = lax.dynamic_slice_in_dim(grad_small_all, me * rows_dev, rows_dev, 0)
    grad_state = grad_small[:, :n_state]
    grad_step = grad_small[:, n_state:]
    n_norm, f_norm, s_norm = adamw(
        norm_gain, grad_norm, first_norm_gain, second_norm_gain, VECTOR_RATE, 0.0
    )
    n_input, f_input, s_input = adamw(
        input_proj, grad_input, first_input_proj, second_input_proj, MATRIX_RATE, WEIGHT_DECAY
    )
    n_state, f_state, s_state = adamw(
        state_proj, grad_state, first_state_proj, second_state_proj, MATRIX_RATE, WEIGHT_DECAY
    )
    n_step, f_step, s_step = adamw(
        step_proj, grad_step, first_step_proj, second_step_proj, MATRIX_RATE, WEIGHT_DECAY
    )
    n_conv, f_conv, s_conv = adamw(
        conv_taps, grad_conv, first_conv_taps, second_conv_taps, VECTOR_RATE, 0.0
    )
    n_head, f_head, s_head = adamw(
        head_coef, grad_coef, first_head_coef, second_head_coef, VECTOR_RATE, 0.0
    )
    n_gated, f_gated, s_gated = adamw(
        gated_gain, grad_gated, first_gated_gain, second_gated_gain, VECTOR_RATE, 0.0
    )
    n_output, f_output, s_output = adamw(
        output_proj, grad_output, first_output_proj, second_output_proj, MATRIX_RATE, WEIGHT_DECAY
    )
    return (
        block_out,
        input_grad,
        grad_norm,
        grad_input,
        grad_state,
        grad_step,
        grad_conv,
        grad_coef,
        grad_gated,
        grad_output,
        n_norm,
        f_norm,
        s_norm,
        n_input,
        f_input,
        s_input,
        n_state,
        f_state,
        s_state,
        n_step,
        f_step,
        s_step,
        n_conv,
        f_conv,
        s_conv,
        n_head,
        f_head,
        s_head,
        n_gated,
        f_gated,
        s_gated,
        n_output,
        f_output,
        s_output,
    )


def solution(mesh):
    return jax.shard_map(
        per_device,
        mesh=mesh,
        in_specs=(
            P(("dp", "row", "col"), None),
            P(("dp", "row", "col"), None),
            P(),
            P(),
            P(),
            P("dp", ("row", "col")),
            P("dp", ("row", "col")),
            P("dp", ("row", "col")),
            P(("dp", "row", "col"), None),
            P(("dp", "row", "col"), None),
            P(("dp", "row", "col"), None),
            P(("dp", "row", "col"), None),
            P(("dp", "row", "col"), None),
            P(("dp", "row", "col"), None),
            P(),
            P(),
            P(),
            P(),
            P(),
            P(),
            P(),
            P(),
            P(),
            P(("row", "col"), "dp"),
            P(("row", "col"), "dp"),
            P(("row", "col"), "dp"),
        ),
        out_specs=(
            P(("dp", "row", "col"), None),
            P(("dp", "row", "col"), None),
            P(),
            P("dp", ("row", "col")),
            P(("dp", "row", "col"), None),
            P(("dp", "row", "col"), None),
            P(),
            P(),
            P(),
            P(("row", "col"), "dp"),
            P(),
            P(),
            P(),
            P("dp", ("row", "col")),
            P("dp", ("row", "col")),
            P("dp", ("row", "col")),
            P(("dp", "row", "col"), None),
            P(("dp", "row", "col"), None),
            P(("dp", "row", "col"), None),
            P(("dp", "row", "col"), None),
            P(("dp", "row", "col"), None),
            P(("dp", "row", "col"), None),
            P(),
            P(),
            P(),
            P(),
            P(),
            P(),
            P(),
            P(),
            P(),
            P(("row", "col"), "dp"),
            P(("row", "col"), "dp"),
            P(("row", "col"), "dp"),
        ),
        check_vma=False,
    )
```

```python
import jax
import jax.numpy as jnp
from jax import lax
from jax.sharding import PartitionSpec as P


SPAN = 256
SEQ_LEN = 1024
ADAM_STEP = 4


PRECISE = lax.Precision.HIGHEST
NORM_EPS = 1e-05
BETA_ONE = 0.9
BETA_TWO = 0.95
ADAM_EPS = 1e-08
MATRIX_RATE = 0.003
VECTOR_RATE = 0.1
WEIGHT_DECAY = 0.1


def causal_conv(values, filters):
    length = values.shape[0]
    padded = jnp.pad(values, ((3, 0), (0, 0)))
    summed = filters[4][None, :] + jnp.zeros_like(values)
    for offset in range(4):
        summed = summed + filters[offset][None, :] * padded[offset : offset + length]
    return summed


def span_scan(values, deltas, rates, key_rows, query_rows):
    length, head_count, head_width = values.shape
    states = key_rows.shape[1]
    blocks = length // SPAN
    values = values.reshape(blocks, SPAN, head_count, head_width)
    deltas = deltas.reshape(blocks, SPAN, head_count)
    key_rows = key_rows.reshape(blocks, SPAN, states)
    query_rows = query_rows.reshape(blocks, SPAN, states)
    lower = (jnp.arange(SPAN)[:, None] >= jnp.arange(SPAN)[None, :]).astype(jnp.float32)
    log_decay = jnp.einsum("qr,krh->kqh", lower, deltas * rates[None, None, :], precision=PRECISE)
    scores = jnp.einsum("kqn,krn->kqr", query_rows, key_rows, precision=PRECISE)
    causal = jnp.arange(SPAN)[:, None] >= jnp.arange(SPAN)[None, :]
    head_decay = jnp.transpose(log_decay, (0, 2, 1))
    head_deltas = jnp.transpose(deltas, (0, 2, 1))
    spread = head_decay[:, :, :, None] - head_decay[:, :, None, :]
    decays = jnp.exp(jnp.where(causal[None, None, :, :], spread, -jnp.inf))
    mixing = scores[:, None, :, :] * decays * head_deltas[:, :, None, :]
    within = jnp.einsum("khqr,krhp->kqhp", mixing, values, precision=PRECISE)
    to_end = jnp.exp(log_decay[:, -1:, :] - log_decay) * deltas
    produced = jnp.einsum("kqn,kqh,kqhp->khnp", key_rows, to_end, values, precision=PRECISE)
    factors = jnp.exp(log_decay[:, -1, :])
    carried = jnp.zeros((head_count, states, head_width), jnp.float32)
    entering = []
    for number in range(blocks):
        entering.append(carried)
        carried = carried * factors[number][:, None, None] + produced[number]
    entering = jnp.stack(entering)
    across = (
        jnp.einsum("kqn,khnp->kqhp", query_rows, entering, precision=PRECISE)
        * jnp.exp(log_decay)[:, :, :, None]
    )
    return (within + across).reshape(length, head_count, head_width)


def mixer_sequence(gate_part, inputs, state_in, step_raw, conv_inner, conv_state, coefs):
    length = inputs.shape[0]
    head_count = coefs.shape[1]
    head_width = inputs.shape[1] // head_count
    state_size = state_in.shape[1] // 2
    conv_out = jax.nn.silu(causal_conv(inputs, conv_inner))
    state_out = jax.nn.silu(causal_conv(state_in, conv_state))
    deltas = jax.nn.softplus(step_raw + coefs[0][None, :])
    rates = -jnp.exp(coefs[1])
    shaped = conv_out.reshape(length, head_count, head_width)
    result = span_scan(shaped, deltas, rates, state_out[:, :state_size], state_out[:, state_size:])
    result = result + coefs[2][None, :, None] * shaped
    return result.reshape(length, head_count * head_width) * jax.nn.silu(gate_part)


def mixer_all(gate_part, inputs, state_in, step_raw, conv_inner, conv_state, coefs):
    seq_count = inputs.shape[0] // SEQ_LEN

    def sequence(pieces):
        return mixer_sequence(
            pieces[0], pieces[1], pieces[2], pieces[3], conv_inner, conv_state, coefs
        )

    gated = lax.map(
        jax.checkpoint(sequence),
        (
            gate_part.reshape(seq_count, SEQ_LEN, -1),
            inputs.reshape(seq_count, SEQ_LEN, -1),
            state_in.reshape(seq_count, SEQ_LEN, -1),
            step_raw.reshape(seq_count, SEQ_LEN, -1),
        ),
    )
    return gated.reshape(inputs.shape[0], -1)


def adamw(weight, gradient, moment_one, moment_two, step_rate, shrink):
    new_one = BETA_ONE * moment_one + (1.0 - BETA_ONE) * gradient
    new_two = BETA_TWO * moment_two + (1.0 - BETA_TWO) * gradient * gradient
    one_hat = new_one / (1.0 - BETA_ONE**ADAM_STEP)
    two_hat = new_two / (1.0 - BETA_TWO**ADAM_STEP)
    updated = weight - step_rate * (one_hat / (jnp.sqrt(two_hat) + ADAM_EPS) + shrink * weight)
    return (updated, new_one, new_two)


def axis_bits(axis):
    return lax.axis_size(axis).bit_length() - 1


def bit_steps(*axes):
    return [(axis, k) for axis in axes for k in range(axis_bits(axis))]


def flip(x, axis, k):
    size = lax.axis_size(axis)
    return lax.ppermute(x, axis, [(j, j ^ (1 << k)) for j in range(size)])


def own_bit(axis, k):
    return (lax.axis_index(axis) >> k) & 1


def sum_bits(x, steps):
    for axis, k in steps:
        x = x + flip(x, axis, k)
    return x


def scatter_bits(x, steps):
    for axis, k in steps:
        b = own_bit(axis, k)
        keep = lax.dynamic_index_in_dim(x, b, 0, keepdims=False)
        send = lax.dynamic_index_in_dim(x, 1 - b, 0, keepdims=False)
        x = keep + flip(send, axis, k)
    return x


def gather_bits(x, steps):
    for axis, k in steps:
        other = flip(x, axis, k)
        x = jnp.where(own_bit(axis, k) == 0, jnp.stack([x, other]), jnp.stack([other, x]))
    return x


def bit_position(axes, step):
    axis, k = step
    below = sum(axis_bits(a) for a in axes[axes.index(axis) + 1 :])
    return below + k


def split_blocks(x, dim, axes, steps):
    total = sum(axis_bits(a) for a in axes)
    shape = x.shape[:dim] + (2,) * total + (x.shape[dim] >> total,) + x.shape[dim + 1 :]
    x = x.reshape(shape)
    front = [dim + total - 1 - bit_position(axes, s) for s in steps]
    rest = [j for j in range(len(shape)) if j not in front]
    return x.transpose(front + rest)


def join_blocks(x, axes, steps):
    total = len(steps)
    order = sorted(range(total), key=lambda j: -bit_position(axes, steps[total - 1 - j]))
    x = x.transpose(order + list(range(total, x.ndim)))
    return x.reshape((-1,) + x.shape[total + 1 :])


def pack_rows(values, width):
    flat = values.reshape(-1)
    rows = -(-flat.shape[0] // width)
    return jnp.pad(flat, (0, rows * width - flat.shape[0])).reshape(rows, width)


def per_device(
    block_in,
    out_grad,
    norm_gain,
    first_norm_gain,
    second_norm_gain,
    input_proj,
    first_input_proj,
    second_input_proj,
    state_proj,
    first_state_proj,
    second_state_proj,
    step_proj,
    first_step_proj,
    second_step_proj,
    conv_taps,
    first_conv_taps,
    second_conv_taps,
    head_coef,
    first_head_coef,
    second_head_coef,
    gated_gain,
    first_gated_gain,
    second_gated_gain,
    output_proj,
    first_output_proj,
    second_output_proj,
):
    groups = lax.axis_size(("row", "col"))
    place = lax.axis_index(("row", "col"))
    tok_dev = block_in.shape[0]
    model = block_in.shape[1]
    group_tok = tok_dev * groups
    inner = gated_gain.shape[0]
    inner_dev = inner // groups
    head_total = head_coef.shape[1]
    heads_dev = head_total // groups
    head_width = inner // head_total
    n_state = state_proj.shape[1]
    n_small = n_state + step_proj.shape[1]
    all_axes = ("dp", "row", "col")
    all_steps = bit_steps(*all_axes)
    dp_steps = bit_steps("dp")
    group_steps = bit_steps("row", "col")
    small = jnp.concatenate([state_proj, step_proj], axis=1).astype(jnp.bfloat16)
    small_full = join_blocks(gather_bits(small, all_steps), all_axes, all_steps)
    in_local = join_blocks(
        gather_bits(input_proj.astype(jnp.bfloat16), dp_steps), ("dp",), dp_steps
    )
    out_parts = gather_bits(output_proj.astype(jnp.bfloat16), dp_steps)
    out_local = jnp.moveaxis(join_blocks(out_parts[..., None, :, :], ("dp",), dp_steps), 0, 1).reshape(
        output_proj.shape[0], -1
    )
    x_float = block_in.astype(jnp.float32)
    inv_rms = lax.rsqrt(jnp.mean(x_float * x_float, axis=1, keepdims=True) + NORM_EPS)
    normed_in = (x_float * inv_rms * norm_gain[None, :]).astype(jnp.bfloat16)
    normed_all = lax.all_gather(normed_in, ("row", "col"), axis=0, tiled=True)
    cotangent = lax.all_gather(out_grad, ("row", "col"), axis=0, tiled=True)
    projected = jnp.dot(normed_all, in_local, preferred_element_type=jnp.float32)
    small_all = jnp.dot(normed_all, small_full, preferred_element_type=jnp.float32).astype(
        jnp.bfloat16
    )
    state_all = small_all[:, :n_state]
    step_all = small_all[:, n_state:]
    paired = projected.reshape(group_tok, heads_dev, 2, head_width)
    gate_part = paired[:, :, 0, :].reshape(group_tok, inner_dev)
    inputs = paired[:, :, 1, :].reshape(group_tok, inner_dev)
    conv_inner = lax.dynamic_slice_in_dim(conv_taps, place * inner_dev, inner_dev, 1)
    conv_state = conv_taps[:, inner:]
    coefs = lax.dynamic_slice_in_dim(head_coef, place * heads_dev, heads_dev, 1)
    step_local = lax.dynamic_slice_in_dim(step_all, place * heads_dev, heads_dev, 1).astype(
        jnp.float32
    )
    gated, mixer_pull = jax.vjp(
        mixer_all,
        gate_part,
        inputs,
        state_all.astype(jnp.float32),
        step_local,
        conv_inner,
        conv_state,
        coefs,
    )
    squares = sum_bits(jnp.sum(gated * gated, axis=1), group_steps)
    gated_rms = lax.rsqrt(squares / inner + NORM_EPS)[:, None]
    gain_local = lax.dynamic_slice_in_dim(gated_gain, place * inner_dev, inner_dev, 0)
    normed_out = (gated * gated_rms * gain_local[None, :]).astype(jnp.bfloat16)
    mixed = lax.psum_scatter(
        jnp.dot(normed_out, out_local, preferred_element_type=jnp.float32),
        ("row", "col"),
        scatter_dimension=0,
        tiled=True,
    )
    block_out = (x_float + mixed).astype(jnp.bfloat16)
    grad_out_local = jnp.einsum(
        "tc,td->cd", normed_out, cotangent, preferred_element_type=jnp.float32
    )
    grad_output = scatter_bits(
        split_blocks(grad_out_local, 1, ("dp",), dp_steps), dp_steps
    )
    d_normed = jnp.einsum("td,cd->tc", cotangent, out_local, preferred_element_type=jnp.float32)
    gain_part = jnp.sum(d_normed * gated * gated_rms, axis=0)
    scaled = d_normed * gain_local[None, :]
    cross = sum_bits(jnp.sum(scaled * gated, axis=1), group_steps)
    d_gated = gated_rms * scaled - gated * gated_rms**3 * (cross / inner)[:, None]
    d_gate, d_inputs, d_state, d_step, d_conv_inner, d_conv_state, d_coefs = mixer_pull(
        d_gated
    )
    d_projected = (
        jnp.stack(
            [
                d_gate.reshape(group_tok, heads_dev, head_width),
                d_inputs.reshape(group_tok, heads_dev, head_width),
            ],
            axis=2,
        )
        .reshape(group_tok, 2 * inner_dev)
        .astype(jnp.bfloat16)
    )
    grad_in_local = jnp.einsum(
        "td,tc->dc", normed_all, d_projected, preferred_element_type=jnp.float32
    )
    step_spread = lax.dynamic_update_slice_in_dim(
        jnp.zeros((group_tok, head_total), jnp.float32), d_step, place * heads_dev, 1
    )
    back_all = lax.psum_scatter(
        jnp.concatenate(
            [
                jnp.einsum("tc,dc->td", d_projected, in_local, preferred_element_type=jnp.float32),
                d_state,
                step_spread,
            ],
            axis=1,
        ),
        ("row", "col"),
        scatter_dimension=0,
        tiled=True,
    )
    d_normed_in = back_all[:, :model]
    small_back = back_all[:, model:].astype(jnp.bfloat16)
    d_normed_in = d_normed_in + jnp.einsum(
        "tc,dc->td", small_back, small_full, preferred_element_type=jnp.float32
    )
    grad_small_part = jnp.einsum(
        "td,tc->dc", normed_in, small_back, preferred_element_type=jnp.float32
    )
    grad_input = scatter_bits(split_blocks(grad_in_local, 0, ("dp",), dp_steps), dp_steps)
    scaled_in = d_normed_in * norm_gain[None, :]
    norm_part = jnp.sum(d_normed_in * x_float * inv_rms, axis=0)
    input_grad = (
        out_grad.astype(jnp.float32)
        + inv_rms * scaled_in
        - x_float * inv_rms**3 * jnp.mean(scaled_in * x_float, axis=1, keepdims=True)
    )
    gated_spread = lax.dynamic_update_slice_in_dim(
        jnp.zeros((inner,), jnp.float32), gain_part, place * inner_dev, 0
    )
    conv_front = lax.dynamic_update_slice_in_dim(
        jnp.zeros((5, inner), jnp.float32), d_conv_inner, place * inner_dev, 1
    )
    conv_spread = jnp.concatenate([conv_front, d_conv_state], axis=1)
    coef_spread = lax.dynamic_update_slice_in_dim(
        jnp.zeros((3, head_total), jnp.float32), d_coefs, place * heads_dev, 1
    )
    pieces = (norm_part, gated_spread, conv_spread, coef_spread)
    offsets = [0]
    for piece in pieces:
        offsets.append(offsets[-1] + piece.size)
    packed = pack_rows(jnp.concatenate([piece.reshape(-1) for piece in pieces]), n_small)
    summed_flat = sum_bits(packed, all_steps).reshape(-1)
    grad_small = scatter_bits(split_blocks(grad_small_part, 0, all_axes, all_steps), all_steps)
    grad_norm, grad_gated, grad_conv, grad_coef = (
        summed_flat[offsets[k] : offsets[k + 1]].reshape(piece.shape)
        for k, piece in enumerate(pieces)
    )
    grad_state = grad_small[:, :n_state]
    grad_step = grad_small[:, n_state:]
    n_norm, f_norm, s_norm = adamw(
        norm_gain, grad_norm, first_norm_gain, second_norm_gain, VECTOR_RATE, 0.0
    )
    n_input, f_input, s_input = adamw(
        input_proj, grad_input, first_input_proj, second_input_proj, MATRIX_RATE, WEIGHT_DECAY
    )
    n_state, f_state, s_state = adamw(
        state_proj, grad_state, first_state_proj, second_state_proj, MATRIX_RATE, WEIGHT_DECAY
    )
    n_step, f_step, s_step = adamw(
        step_proj, grad_step, first_step_proj, second_step_proj, MATRIX_RATE, WEIGHT_DECAY
    )
    n_conv, f_conv, s_conv = adamw(
        conv_taps, grad_conv, first_conv_taps, second_conv_taps, VECTOR_RATE, 0.0
    )
    n_head, f_head, s_head = adamw(
        head_coef, grad_coef, first_head_coef, second_head_coef, VECTOR_RATE, 0.0
    )
    n_gated, f_gated, s_gated = adamw(
        gated_gain, grad_gated, first_gated_gain, second_gated_gain, VECTOR_RATE, 0.0
    )
    n_output, f_output, s_output = adamw(
        output_proj, grad_output, first_output_proj, second_output_proj, MATRIX_RATE, WEIGHT_DECAY
    )
    return (
        block_out,
        input_grad,
        grad_norm,
        grad_input,
        grad_state,
        grad_step,
        grad_conv,
        grad_coef,
        grad_gated,
        grad_output,
        n_norm,
        f_norm,
        s_norm,
        n_input,
        f_input,
        s_input,
        n_state,
        f_state,
        s_state,
        n_step,
        f_step,
        s_step,
        n_conv,
        f_conv,
        s_conv,
        n_head,
        f_head,
        s_head,
        n_gated,
        f_gated,
        s_gated,
        n_output,
        f_output,
        s_output,
    )


def solution(mesh):
    return jax.shard_map(
        per_device,
        mesh=mesh,
        in_specs=(
            P(("dp", "row", "col"), None),
            P(("dp", "row", "col"), None),
            P(),
            P(),
            P(),
            P("dp", ("row", "col")),
            P("dp", ("row", "col")),
            P("dp", ("row", "col")),
            P(("dp", "row", "col"), None),
            P(("dp", "row", "col"), None),
            P(("dp", "row", "col"), None),
            P(("dp", "row", "col"), None),
            P(("dp", "row", "col"), None),
            P(("dp", "row", "col"), None),
            P(),
            P(),
            P(),
            P(),
            P(),
            P(),
            P(),
            P(),
            P(),
            P(("row", "col"), "dp"),
            P(("row", "col"), "dp"),
            P(("row", "col"), "dp"),
        ),
        out_specs=(
            P(("dp", "row", "col"), None),
            P(("dp", "row", "col"), None),
            P(),
            P("dp", ("row", "col")),
            P(("dp", "row", "col"), None),
            P(("dp", "row", "col"), None),
            P(),
            P(),
            P(),
            P(("row", "col"), "dp"),
            P(),
            P(),
            P(),
            P("dp", ("row", "col")),
            P("dp", ("row", "col")),
            P("dp", ("row", "col")),
            P(("dp", "row", "col"), None),
            P(("dp", "row", "col"), None),
            P(("dp", "row", "col"), None),
            P(("dp", "row", "col"), None),
            P(("dp", "row", "col"), None),
            P(("dp", "row", "col"), None),
            P(),
            P(),
            P(),
            P(),
            P(),
            P(),
            P(),
            P(),
            P(),
            P(("row", "col"), "dp"),
            P(("row", "col"), "dp"),
            P(("row", "col"), "dp"),
        ),
        check_vma=False,
    )
```

```python
import jax
import jax.numpy as jnp
from jax import lax
from jax.sharding import PartitionSpec as P


SPAN = 256
SEQ_LEN = 1024
ADAM_STEP = 4


PRECISE = lax.Precision.HIGHEST
NORM_EPS = 1e-05
BETA_ONE = 0.9
BETA_TWO = 0.95
ADAM_EPS = 1e-08
MATRIX_RATE = 0.003
VECTOR_RATE = 0.1
WEIGHT_DECAY = 0.1


def causal_conv(values, filters):
    length = values.shape[0]
    padded = jnp.pad(values, ((3, 0), (0, 0)))
    summed = filters[4][None, :] + jnp.zeros_like(values)
    for offset in range(4):
        summed = summed + filters[offset][None, :] * padded[offset : offset + length]
    return summed


def span_scan(values, deltas, rates, key_rows, query_rows):
    length, head_count, head_width = values.shape
    states = key_rows.shape[1]
    blocks = length // SPAN
    values = values.reshape(blocks, SPAN, head_count, head_width)
    deltas = deltas.reshape(blocks, SPAN, head_count)
    key_rows = key_rows.reshape(blocks, SPAN, states)
    query_rows = query_rows.reshape(blocks, SPAN, states)
    lower = (jnp.arange(SPAN)[:, None] >= jnp.arange(SPAN)[None, :]).astype(jnp.float32)
    log_decay = jnp.einsum("qr,krh->kqh", lower, deltas * rates[None, None, :], precision=PRECISE)
    scores = jnp.einsum("kqn,krn->kqr", query_rows, key_rows, precision=PRECISE)
    causal = jnp.arange(SPAN)[:, None] >= jnp.arange(SPAN)[None, :]
    head_decay = jnp.transpose(log_decay, (0, 2, 1))
    head_deltas = jnp.transpose(deltas, (0, 2, 1))
    spread = head_decay[:, :, :, None] - head_decay[:, :, None, :]
    decays = jnp.exp(jnp.where(causal[None, None, :, :], spread, -jnp.inf))
    mixing = scores[:, None, :, :] * decays * head_deltas[:, :, None, :]
    within = jnp.einsum("khqr,krhp->kqhp", mixing, values, precision=PRECISE)
    to_end = jnp.exp(log_decay[:, -1:, :] - log_decay) * deltas
    produced = jnp.einsum("kqn,kqh,kqhp->khnp", key_rows, to_end, values, precision=PRECISE)
    factors = jnp.exp(log_decay[:, -1, :])
    carried = jnp.zeros((head_count, states, head_width), jnp.float32)
    entering = []
    for number in range(blocks):
        entering.append(carried)
        carried = carried * factors[number][:, None, None] + produced[number]
    entering = jnp.stack(entering)
    across = (
        jnp.einsum("kqn,khnp->kqhp", query_rows, entering, precision=PRECISE)
        * jnp.exp(log_decay)[:, :, :, None]
    )
    return (within + across).reshape(length, head_count, head_width)


def mixer_sequence(gate_part, inputs, state_in, step_raw, conv_inner, conv_state, coefs):
    length = inputs.shape[0]
    head_count = coefs.shape[1]
    head_width = inputs.shape[1] // head_count
    state_size = state_in.shape[1] // 2
    conv_out = jax.nn.silu(causal_conv(inputs, conv_inner))
    state_out = jax.nn.silu(causal_conv(state_in, conv_state))
    deltas = jax.nn.softplus(step_raw + coefs[0][None, :])
    rates = -jnp.exp(coefs[1])
    shaped = conv_out.reshape(length, head_count, head_width)
    result = span_scan(shaped, deltas, rates, state_out[:, :state_size], state_out[:, state_size:])
    result = result + coefs[2][None, :, None] * shaped
    return result.reshape(length, head_count * head_width) * jax.nn.silu(gate_part)


def mixer_all(gate_part, inputs, state_in, step_raw, conv_inner, conv_state, coefs):
    seq_count = inputs.shape[0] // SEQ_LEN

    def sequence(pieces):
        return mixer_sequence(
            pieces[0], pieces[1], pieces[2], pieces[3], conv_inner, conv_state, coefs
        )

    gated = lax.map(
        jax.checkpoint(sequence),
        (
            gate_part.reshape(seq_count, SEQ_LEN, -1),
            inputs.reshape(seq_count, SEQ_LEN, -1),
            state_in.reshape(seq_count, SEQ_LEN, -1),
            step_raw.reshape(seq_count, SEQ_LEN, -1),
        ),
    )
    return gated.reshape(inputs.shape[0], -1)


def adamw(weight, gradient, moment_one, moment_two, step_rate, shrink):
    new_one = BETA_ONE * moment_one + (1.0 - BETA_ONE) * gradient
    new_two = BETA_TWO * moment_two + (1.0 - BETA_TWO) * gradient * gradient
    one_hat = new_one / (1.0 - BETA_ONE**ADAM_STEP)
    two_hat = new_two / (1.0 - BETA_TWO**ADAM_STEP)
    updated = weight - step_rate * (one_hat / (jnp.sqrt(two_hat) + ADAM_EPS) + shrink * weight)
    return (updated, new_one, new_two)


def axis_bits(axis):
    return lax.axis_size(axis).bit_length() - 1


def bit_steps(*axes):
    return [(axis, k) for axis in axes for k in range(axis_bits(axis))]


def flip(x, axis, k):
    size = lax.axis_size(axis)
    return lax.ppermute(x, axis, [(j, j ^ (1 << k)) for j in range(size)])


def own_bit(axis, k):
    return (lax.axis_index(axis) >> k) & 1


def sum_bits(x, steps):
    for axis, k in steps:
        x = x + flip(x, axis, k)
    return x


def scatter_bits(x, steps):
    for axis, k in steps:
        b = own_bit(axis, k)
        keep = lax.dynamic_index_in_dim(x, b, 0, keepdims=False)
        send = lax.dynamic_index_in_dim(x, 1 - b, 0, keepdims=False)
        x = keep + flip(send, axis, k)
    return x


def gather_bits(x, steps):
    for axis, k in steps:
        other = flip(x, axis, k)
        x = jnp.where(own_bit(axis, k) == 0, jnp.stack([x, other]), jnp.stack([other, x]))
    return x


def bit_position(axes, step):
    axis, k = step
    below = sum(axis_bits(a) for a in axes[axes.index(axis) + 1 :])
    return below + k


def split_blocks(x, dim, axes, steps):
    total = sum(axis_bits(a) for a in axes)
    shape = x.shape[:dim] + (2,) * total + (x.shape[dim] >> total,) + x.shape[dim + 1 :]
    x = x.reshape(shape)
    front = [dim + total - 1 - bit_position(axes, s) for s in steps]
    rest = [j for j in range(len(shape)) if j not in front]
    return x.transpose(front + rest)


def join_blocks(x, axes, steps):
    total = len(steps)
    order = sorted(range(total), key=lambda j: -bit_position(axes, steps[total - 1 - j]))
    x = x.transpose(order + list(range(total, x.ndim)))
    return x.reshape((-1,) + x.shape[total + 1 :])


def pack_rows(values, width):
    flat = values.reshape(-1)
    rows = -(-flat.shape[0] // width)
    return jnp.pad(flat, (0, rows * width - flat.shape[0])).reshape(rows, width)


def per_device(
    block_in,
    out_grad,
    norm_gain,
    first_norm_gain,
    second_norm_gain,
    input_proj,
    first_input_proj,
    second_input_proj,
    state_proj,
    first_state_proj,
    second_state_proj,
    step_proj,
    first_step_proj,
    second_step_proj,
    conv_taps,
    first_conv_taps,
    second_conv_taps,
    head_coef,
    first_head_coef,
    second_head_coef,
    gated_gain,
    first_gated_gain,
    second_gated_gain,
    output_proj,
    first_output_proj,
    second_output_proj,
):
    groups = lax.axis_size(("row", "col"))
    place = lax.axis_index(("row", "col"))
    tok_dev = block_in.shape[0]
    model = block_in.shape[1]
    group_tok = tok_dev * groups
    inner = gated_gain.shape[0]
    inner_dev = inner // groups
    head_total = head_coef.shape[1]
    heads_dev = head_total // groups
    head_width = inner // head_total
    n_state = state_proj.shape[1]
    n_small = n_state + step_proj.shape[1]
    rows_dev = state_proj.shape[0]
    in_rows, in_cols = input_proj.shape
    all_axes = ("dp", "row", "col")
    all_steps = bit_steps(*all_axes)
    dp_steps = bit_steps("dp")
    group_steps = bit_steps("row", "col")
    small = jnp.concatenate([state_proj, step_proj], axis=1).astype(jnp.bfloat16)
    out_rows, out_cols = output_proj.shape
    both = gather_bits(
        jnp.concatenate(
            [
                input_proj.astype(jnp.bfloat16),
                pack_rows(output_proj.astype(jnp.bfloat16), in_cols),
            ],
            axis=0,
        ),
        dp_steps,
    )
    lead = both.shape[: len(dp_steps)]
    in_local = join_blocks(both[..., :in_rows, :], ("dp",), dp_steps)
    out_parts = both[..., in_rows:, :].reshape(lead + (-1,))[..., : out_rows * out_cols]
    out_local = jnp.moveaxis(
        join_blocks(out_parts.reshape(lead + (1, out_rows, out_cols)), ("dp",), dp_steps), 0, 1
    ).reshape(out_rows, -1)
    x_float = block_in.astype(jnp.float32)
    inv_rms = lax.rsqrt(jnp.mean(x_float * x_float, axis=1, keepdims=True) + NORM_EPS)
    normed_in = (x_float * inv_rms * norm_gain[None, :]).astype(jnp.bfloat16)
    tokens = lax.all_gather(
        jnp.concatenate([normed_in, pack_rows(small, model)], axis=0), ("row", "col"), axis=0
    )
    normed_all = tokens[:, :tok_dev].reshape(group_tok, model)
    small_group = (
        tokens[:, tok_dev:].reshape(groups, -1)[:, : rows_dev * n_small].reshape(-1, n_small)
    )
    small_full = join_blocks(gather_bits(small_group, dp_steps), ("dp",), dp_steps)
    cotangent = lax.all_gather(out_grad, ("row", "col"), axis=0, tiled=True)
    projected = jnp.dot(normed_all, in_local, preferred_element_type=jnp.float32)
    small_all = jnp.dot(normed_all, small_full, preferred_element_type=jnp.float32).astype(
        jnp.bfloat16
    )
    state_all = small_all[:, :n_state]
    step_all = small_all[:, n_state:]
    paired = projected.reshape(group_tok, heads_dev, 2, head_width)
    gate_part = paired[:, :, 0, :].reshape(group_tok, inner_dev)
    inputs = paired[:, :, 1, :].reshape(group_tok, inner_dev)
    conv_inner = lax.dynamic_slice_in_dim(conv_taps, place * inner_dev, inner_dev, 1)
    conv_state = conv_taps[:, inner:]
    coefs = lax.dynamic_slice_in_dim(head_coef, place * heads_dev, heads_dev, 1)
    step_local = lax.dynamic_slice_in_dim(step_all, place * heads_dev, heads_dev, 1).astype(
        jnp.float32
    )
    gated, mixer_pull = jax.vjp(
        mixer_all,
        gate_part,
        inputs,
        state_all.astype(jnp.float32),
        step_local,
        conv_inner,
        conv_state,
        coefs,
    )
    squares = sum_bits(jnp.sum(gated * gated, axis=1), group_steps)
    gated_rms = lax.rsqrt(squares / inner + NORM_EPS)[:, None]
    gain_local = lax.dynamic_slice_in_dim(gated_gain, place * inner_dev, inner_dev, 0)
    normed_out = (gated * gated_rms * gain_local[None, :]).astype(jnp.bfloat16)
    mixed = lax.psum_scatter(
        jnp.dot(normed_out, out_local, preferred_element_type=jnp.float32),
        ("row", "col"),
        scatter_dimension=0,
        tiled=True,
    )
    block_out = (x_float + mixed).astype(jnp.bfloat16)
    grad_out_local = jnp.einsum(
        "tc,td->cd", normed_out, cotangent, preferred_element_type=jnp.float32
    )
    grad_output = scatter_bits(
        split_blocks(grad_out_local, 1, ("dp",), dp_steps), dp_steps
    )
    d_normed = jnp.einsum("td,cd->tc", cotangent, out_local, preferred_element_type=jnp.float32)
    gain_part = jnp.sum(d_normed * gated * gated_rms, axis=0)
    scaled = d_normed * gain_local[None, :]
    cross = sum_bits(jnp.sum(scaled * gated, axis=1), group_steps)
    d_gated = gated_rms * scaled - gated * gated_rms**3 * (cross / inner)[:, None]
    d_gate, d_inputs, d_state, d_step, d_conv_inner, d_conv_state, d_coefs = mixer_pull(
        d_gated
    )
    d_projected = (
        jnp.stack(
            [
                d_gate.reshape(group_tok, heads_dev, head_width),
                d_inputs.reshape(group_tok, heads_dev, head_width),
            ],
            axis=2,
        )
        .reshape(group_tok, 2 * inner_dev)
        .astype(jnp.bfloat16)
    )
    grad_in_local = jnp.einsum(
        "td,tc->dc", normed_all, d_projected, preferred_element_type=jnp.float32
    )
    step_spread = jnp.where(
        (jnp.arange(head_total) // heads_dev == place)[None, :],
        jnp.tile(d_step, (1, groups)),
        0.0,
    )
    back_all = lax.psum_scatter(
        jnp.concatenate(
            [
                jnp.einsum("tc,dc->td", d_projected, in_local, preferred_element_type=jnp.float32),
                d_state,
                step_spread,
            ],
            axis=1,
        ),
        ("row", "col"),
        scatter_dimension=0,
        tiled=True,
    )
    d_normed_in = back_all[:, :model]
    small_back = back_all[:, model:].astype(jnp.bfloat16)
    d_normed_in = d_normed_in + jnp.einsum(
        "tc,dc->td", small_back, small_full, preferred_element_type=jnp.float32
    )
    grad_small_part = jnp.einsum(
        "td,tc->dc", normed_in, small_back, preferred_element_type=jnp.float32
    )
    grad_input = scatter_bits(split_blocks(grad_in_local, 0, ("dp",), dp_steps), dp_steps)
    scaled_in = d_normed_in * norm_gain[None, :]
    norm_part = jnp.sum(d_normed_in * x_float * inv_rms, axis=0)
    input_grad = (
        out_grad.astype(jnp.float32)
        + inv_rms * scaled_in
        - x_float * inv_rms**3 * jnp.mean(scaled_in * x_float, axis=1, keepdims=True)
    )
    gated_spread = lax.dynamic_update_slice_in_dim(
        jnp.zeros((inner,), jnp.float32), gain_part, place * inner_dev, 0
    )
    conv_front = lax.dynamic_update_slice_in_dim(
        jnp.zeros((5, inner), jnp.float32), d_conv_inner, place * inner_dev, 1
    )
    conv_spread = jnp.concatenate([conv_front, d_conv_state], axis=1)
    coef_spread = lax.dynamic_update_slice_in_dim(
        jnp.zeros((3, head_total), jnp.float32), d_coefs, place * heads_dev, 1
    )
    pieces = (norm_part, gated_spread, conv_spread, coef_spread)
    offsets = [0]
    for piece in pieces:
        offsets.append(offsets[-1] + piece.size)
    packed = pack_rows(jnp.concatenate([piece.reshape(-1) for piece in pieces]), n_small)
    summed_flat = sum_bits(packed, all_steps).reshape(-1)
    grad_small = scatter_bits(split_blocks(grad_small_part, 0, all_axes, all_steps), all_steps)
    grad_norm, grad_gated, grad_conv, grad_coef = (
        summed_flat[offsets[k] : offsets[k + 1]].reshape(piece.shape)
        for k, piece in enumerate(pieces)
    )
    grad_state = grad_small[:, :n_state]
    grad_step = grad_small[:, n_state:]
    n_norm, f_norm, s_norm = adamw(
        norm_gain, grad_norm, first_norm_gain, second_norm_gain, VECTOR_RATE, 0.0
    )
    n_input, f_input, s_input = adamw(
        input_proj, grad_input, first_input_proj, second_input_proj, MATRIX_RATE, WEIGHT_DECAY
    )
    n_state, f_state, s_state = adamw(
        state_proj, grad_state, first_state_proj, second_state_proj, MATRIX_RATE, WEIGHT_DECAY
    )
    n_step, f_step, s_step = adamw(
        step_proj, grad_step, first_step_proj, second_step_proj, MATRIX_RATE, WEIGHT_DECAY
    )
    n_conv, f_conv, s_conv = adamw(
        conv_taps, grad_conv, first_conv_taps, second_conv_taps, VECTOR_RATE, 0.0
    )
    n_head, f_head, s_head = adamw(
        head_coef, grad_coef, first_head_coef, second_head_coef, VECTOR_RATE, 0.0
    )
    n_gated, f_gated, s_gated = adamw(
        gated_gain, grad_gated, first_gated_gain, second_gated_gain, VECTOR_RATE, 0.0
    )
    n_output, f_output, s_output = adamw(
        output_proj, grad_output, first_output_proj, second_output_proj, MATRIX_RATE, WEIGHT_DECAY
    )
    return (
        block_out,
        input_grad,
        grad_norm,
        grad_input,
        grad_state,
        grad_step,
        grad_conv,
        grad_coef,
        grad_gated,
        grad_output,
        n_norm,
        f_norm,
        s_norm,
        n_input,
        f_input,
        s_input,
        n_state,
        f_state,
        s_state,
        n_step,
        f_step,
        s_step,
        n_conv,
        f_conv,
        s_conv,
        n_head,
        f_head,
        s_head,
        n_gated,
        f_gated,
        s_gated,
        n_output,
        f_output,
        s_output,
    )


def solution(mesh):
    return jax.shard_map(
        per_device,
        mesh=mesh,
        in_specs=(
            P(("dp", "row", "col"), None),
            P(("dp", "row", "col"), None),
            P(),
            P(),
            P(),
            P("dp", ("row", "col")),
            P("dp", ("row", "col")),
            P("dp", ("row", "col")),
            P(("dp", "row", "col"), None),
            P(("dp", "row", "col"), None),
            P(("dp", "row", "col"), None),
            P(("dp", "row", "col"), None),
            P(("dp", "row", "col"), None),
            P(("dp", "row", "col"), None),
            P(),
            P(),
            P(),
            P(),
            P(),
            P(),
            P(),
            P(),
            P(),
            P(("row", "col"), "dp"),
            P(("row", "col"), "dp"),
            P(("row", "col"), "dp"),
        ),
        out_specs=(
            P(("dp", "row", "col"), None),
            P(("dp", "row", "col"), None),
            P(),
            P("dp", ("row", "col")),
            P(("dp", "row", "col"), None),
            P(("dp", "row", "col"), None),
            P(),
            P(),
            P(),
            P(("row", "col"), "dp"),
            P(),
            P(),
            P(),
            P("dp", ("row", "col")),
            P("dp", ("row", "col")),
            P("dp", ("row", "col")),
            P(("dp", "row", "col"), None),
            P(("dp", "row", "col"), None),
            P(("dp", "row", "col"), None),
            P(("dp", "row", "col"), None),
            P(("dp", "row", "col"), None),
            P(("dp", "row", "col"), None),
            P(),
            P(),
            P(),
            P(),
            P(),
            P(),
            P(),
            P(),
            P(),
            P(("row", "col"), "dp"),
            P(("row", "col"), "dp"),
            P(("row", "col"), "dp"),
        ),
        check_vma=False,
    )
```

```python
import jax
import jax.numpy as jnp
from jax import lax
from jax.sharding import PartitionSpec as P


SPAN = 256
SEQ_LEN = 1024
ADAM_STEP = 4


PRECISE = lax.Precision.HIGHEST
NORM_EPS = 1e-05
BETA_ONE = 0.9
BETA_TWO = 0.95
ADAM_EPS = 1e-08
MATRIX_RATE = 0.003
VECTOR_RATE = 0.1
WEIGHT_DECAY = 0.1


def causal_conv(values, filters):
    length = values.shape[0]
    padded = jnp.pad(values, ((3, 0), (0, 0)))
    summed = filters[4][None, :] + jnp.zeros_like(values)
    for offset in range(4):
        summed = summed + filters[offset][None, :] * padded[offset : offset + length]
    return summed


def span_scan(values, deltas, rates, key_rows, query_rows):
    length, head_count, head_width = values.shape
    states = key_rows.shape[1]
    blocks = length // SPAN
    values = values.reshape(blocks, SPAN, head_count, head_width)
    deltas = deltas.reshape(blocks, SPAN, head_count)
    key_rows = key_rows.reshape(blocks, SPAN, states)
    query_rows = query_rows.reshape(blocks, SPAN, states)
    lower = (jnp.arange(SPAN)[:, None] >= jnp.arange(SPAN)[None, :]).astype(jnp.float32)
    log_decay = jnp.einsum("qr,krh->kqh", lower, deltas * rates[None, None, :], precision=PRECISE)
    scores = jnp.einsum("kqn,krn->kqr", query_rows, key_rows, precision=PRECISE)
    causal = jnp.arange(SPAN)[:, None] >= jnp.arange(SPAN)[None, :]
    head_decay = jnp.transpose(log_decay, (0, 2, 1))
    head_deltas = jnp.transpose(deltas, (0, 2, 1))
    spread = head_decay[:, :, :, None] - head_decay[:, :, None, :]
    decays = jnp.exp(jnp.where(causal[None, None, :, :], spread, -jnp.inf))
    mixing = scores[:, None, :, :] * decays * head_deltas[:, :, None, :]
    within = jnp.einsum("khqr,krhp->kqhp", mixing, values, precision=PRECISE)
    to_end = jnp.exp(log_decay[:, -1:, :] - log_decay) * deltas
    produced = jnp.einsum("kqn,kqh,kqhp->khnp", key_rows, to_end, values, precision=PRECISE)
    factors = jnp.exp(log_decay[:, -1, :])
    carried = jnp.zeros((head_count, states, head_width), jnp.float32)
    entering = []
    for number in range(blocks):
        entering.append(carried)
        carried = carried * factors[number][:, None, None] + produced[number]
    entering = jnp.stack(entering)
    across = (
        jnp.einsum("kqn,khnp->kqhp", query_rows, entering, precision=PRECISE)
        * jnp.exp(log_decay)[:, :, :, None]
    )
    return (within + across).reshape(length, head_count, head_width)


def mixer_sequence(gate_part, inputs, state_in, step_raw, conv_inner, conv_state, coefs):
    length = inputs.shape[0]
    head_count = coefs.shape[1]
    head_width = inputs.shape[1] // head_count
    state_size = state_in.shape[1] // 2
    conv_out = jax.nn.silu(causal_conv(inputs, conv_inner))
    state_out = jax.nn.silu(causal_conv(state_in, conv_state))
    deltas = jax.nn.softplus(step_raw + coefs[0][None, :])
    rates = -jnp.exp(coefs[1])
    shaped = conv_out.reshape(length, head_count, head_width)
    result = span_scan(shaped, deltas, rates, state_out[:, :state_size], state_out[:, state_size:])
    result = result + coefs[2][None, :, None] * shaped
    return result.reshape(length, head_count * head_width) * jax.nn.silu(gate_part)


def mixer_all(gate_part, inputs, state_in, step_raw, conv_inner, conv_state, coefs):
    seq_count = inputs.shape[0] // SEQ_LEN

    def sequence(pieces):
        return mixer_sequence(
            pieces[0], pieces[1], pieces[2], pieces[3], conv_inner, conv_state, coefs
        )

    gated = lax.map(
        jax.checkpoint(sequence),
        (
            gate_part.reshape(seq_count, SEQ_LEN, -1),
            inputs.reshape(seq_count, SEQ_LEN, -1),
            state_in.reshape(seq_count, SEQ_LEN, -1),
            step_raw.reshape(seq_count, SEQ_LEN, -1),
        ),
    )
    return gated.reshape(inputs.shape[0], -1)


def adamw(weight, gradient, moment_one, moment_two, step_rate, shrink):
    new_one = BETA_ONE * moment_one + (1.0 - BETA_ONE) * gradient
    new_two = BETA_TWO * moment_two + (1.0 - BETA_TWO) * gradient * gradient
    one_hat = new_one / (1.0 - BETA_ONE**ADAM_STEP)
    two_hat = new_two / (1.0 - BETA_TWO**ADAM_STEP)
    updated = weight - step_rate * (one_hat / (jnp.sqrt(two_hat) + ADAM_EPS) + shrink * weight)
    return (updated, new_one, new_two)


def axis_bits(axis):
    return lax.axis_size(axis).bit_length() - 1


def bit_steps(*axes):
    return [(axis, k) for axis in axes for k in range(axis_bits(axis))]


def flip(x, axis, k):
    size = lax.axis_size(axis)
    return lax.ppermute(x, axis, [(j, j ^ (1 << k)) for j in range(size)])


def own_bit(axis, k):
    return (lax.axis_index(axis) >> k) & 1


def sum_bits(x, steps):
    for axis, k in steps:
        x = x + flip(x, axis, k)
    return x


def scatter_bits(x, steps):
    for axis, k in steps:
        b = own_bit(axis, k)
        keep = lax.dynamic_index_in_dim(x, b, 0, keepdims=False)
        send = lax.dynamic_index_in_dim(x, 1 - b, 0, keepdims=False)
        x = keep + flip(send, axis, k)
    return x


def gather_bits(x, steps):
    for axis, k in steps:
        other = flip(x, axis, k)
        x = jnp.where(own_bit(axis, k) == 0, jnp.stack([x, other]), jnp.stack([other, x]))
    return x


def bit_position(axes, step):
    axis, k = step
    below = sum(axis_bits(a) for a in axes[axes.index(axis) + 1 :])
    return below + k


def split_blocks(x, dim, axes, steps):
    total = sum(axis_bits(a) for a in axes)
    shape = x.shape[:dim] + (2,) * total + (x.shape[dim] >> total,) + x.shape[dim + 1 :]
    x = x.reshape(shape)
    front = [dim + total - 1 - bit_position(axes, s) for s in steps]
    rest = [j for j in range(len(shape)) if j not in front]
    return x.transpose(front + rest)


def pack_rows(values, width):
    flat = values.reshape(-1)
    rows = -(-flat.shape[0] // width)
    return jnp.pad(flat, (0, rows * width - flat.shape[0])).reshape(rows, width)


def two_blocks(values, first, second, width, axis):
    return jnp.concatenate(
        [
            lax.dynamic_slice_in_dim(values, first * width, width, axis),
            lax.dynamic_slice_in_dim(values, second * width, width, axis),
        ],
        axis=axis,
    )


def spread_two(values, first, second, width, total, axis):
    reps = [1] * values.ndim
    reps[axis] = total // width
    block = (jnp.arange(total) // width).reshape([-1 if k == axis else 1 for k in range(values.ndim)])
    low = jnp.tile(lax.slice_in_dim(values, 0, width, axis=axis), reps)
    high = jnp.tile(lax.slice_in_dim(values, width, 2 * width, axis=axis), reps)
    return jnp.where(block == first, low, jnp.where(block == second, high, 0.0))


def per_device(
    block_in,
    out_grad,
    norm_gain,
    first_norm_gain,
    second_norm_gain,
    input_proj,
    first_input_proj,
    second_input_proj,
    state_proj,
    first_state_proj,
    second_state_proj,
    step_proj,
    first_step_proj,
    second_step_proj,
    conv_taps,
    first_conv_taps,
    second_conv_taps,
    head_coef,
    first_head_coef,
    second_head_coef,
    gated_gain,
    first_gated_gain,
    second_gated_gain,
    output_proj,
    first_output_proj,
    second_output_proj,
):
    groups = lax.axis_size(("row", "col"))
    cols = lax.axis_size("col")
    rows = lax.axis_size("row")
    col = lax.axis_index("col")
    tok_dev = block_in.shape[0]
    model = block_in.shape[1]
    seq_tok = tok_dev * cols
    inner = gated_gain.shape[0]
    inner_dev = inner // groups
    head_total = head_coef.shape[1]
    heads_dev = head_total // groups
    head_width = inner // head_total
    n_state = state_proj.shape[1]
    n_small = n_state + step_proj.shape[1]
    rows_dev = state_proj.shape[0]
    in_rows, in_cols = input_proj.shape
    out_rows, out_cols = output_proj.shape
    low_block = col
    high_block = col + cols * (rows - 1)
    all_axes = ("dp", "row", "col")
    all_steps = bit_steps(*all_axes)
    dp_steps = bit_steps("dp")
    row_steps = bit_steps("row")
    col_steps = bit_steps("col")
    nd = len(dp_steps)
    small = jnp.concatenate([state_proj, step_proj], axis=1).astype(jnp.bfloat16)
    both = gather_bits(
        jnp.concatenate(
            [
                input_proj.astype(jnp.bfloat16),
                pack_rows(output_proj.astype(jnp.bfloat16), in_cols),
            ],
            axis=0,
        ),
        dp_steps + row_steps,
    )
    lead = both.shape[: nd + 1]
    win = both[..., :in_rows, :]
    in_local = jnp.moveaxis(win, 0, nd + 1).reshape((1 << nd) * in_rows, rows * in_cols)
    wout = both[..., in_rows:, :].reshape(lead + (-1,))[..., : out_rows * out_cols]
    wout = wout.reshape(lead + (out_rows, out_cols))
    out_local = jnp.moveaxis(wout, nd + 1, 1).reshape(rows * out_rows, (1 << nd) * out_cols)
    x_float = block_in.astype(jnp.float32)
    inv_rms = lax.rsqrt(jnp.mean(x_float * x_float, axis=1, keepdims=True) + NORM_EPS)
    normed_in = (x_float * inv_rms * norm_gain[None, :]).astype(jnp.bfloat16)
    tokens = lax.all_gather(
        jnp.concatenate([normed_in, pack_rows(small, model)], axis=0), "col", axis=0
    )
    normed_all = tokens[:, :tok_dev].reshape(seq_tok, model)
    small_col = tokens[:, tok_dev:].reshape(cols, -1)[:, : rows_dev * n_small].reshape(-1, n_small)
    small_full = gather_bits(small_col, row_steps + dp_steps).reshape(-1, n_small)
    cotangent = lax.all_gather(out_grad, "col", axis=0, tiled=True)
    projected = jnp.dot(normed_all, in_local, preferred_element_type=jnp.float32)
    small_all = jnp.dot(normed_all, small_full, preferred_element_type=jnp.float32).astype(
        jnp.bfloat16
    )
    state_all = small_all[:, :n_state]
    step_all = small_all[:, n_state:]
    local_heads = 2 * heads_dev
    local_inner = 2 * inner_dev
    paired = projected.reshape(seq_tok, local_heads, 2, head_width)
    gate_part = paired[:, :, 0, :].reshape(seq_tok, local_inner)
    inputs = paired[:, :, 1, :].reshape(seq_tok, local_inner)
    conv_inner = two_blocks(conv_taps[:, :inner], low_block, high_block, inner_dev, 1)
    conv_state = conv_taps[:, inner:]
    coefs = two_blocks(head_coef, low_block, high_block, heads_dev, 1)
    step_local = two_blocks(step_all, low_block, high_block, heads_dev, 1).astype(jnp.float32)
    gated, mixer_pull = jax.vjp(
        mixer_all,
        gate_part,
        inputs,
        state_all.astype(jnp.float32),
        step_local,
        conv_inner,
        conv_state,
        coefs,
    )
    squares = sum_bits(jnp.sum(gated * gated, axis=1), col_steps)
    gated_rms = lax.rsqrt(squares / inner + NORM_EPS)[:, None]
    gain_local = two_blocks(gated_gain, low_block, high_block, inner_dev, 0)
    normed_out = (gated * gated_rms * gain_local[None, :]).astype(jnp.bfloat16)
    mixed = lax.psum_scatter(
        jnp.dot(normed_out, out_local, preferred_element_type=jnp.float32),
        "col",
        scatter_dimension=0,
        tiled=True,
    )
    block_out = (x_float + mixed).astype(jnp.bfloat16)
    grad_out_local = jnp.einsum(
        "tc,td->cd", normed_out, cotangent, preferred_element_type=jnp.float32
    )
    parts = grad_out_local.reshape((rows, out_rows) + (2,) * nd + (out_cols,))
    parts = parts.transpose(tuple(range(nd + 1, 1, -1)) + (0, 1, nd + 2))
    grad_output = scatter_bits(parts, dp_steps + row_steps)
    d_normed = jnp.einsum("td,cd->tc", cotangent, out_local, preferred_element_type=jnp.float32)
    gain_part = jnp.sum(d_normed * gated * gated_rms, axis=0)
    scaled = d_normed * gain_local[None, :]
    cross = sum_bits(jnp.sum(scaled * gated, axis=1), col_steps)
    d_gated = gated_rms * scaled - gated * gated_rms**3 * (cross / inner)[:, None]
    d_gate, d_inputs, d_state, d_step, d_conv_inner, d_conv_state, d_coefs = mixer_pull(
        d_gated
    )
    d_projected = (
        jnp.stack(
            [
                d_gate.reshape(seq_tok, local_heads, head_width),
                d_inputs.reshape(seq_tok, local_heads, head_width),
            ],
            axis=2,
        )
        .reshape(seq_tok, 2 * local_inner)
        .astype(jnp.bfloat16)
    )
    grad_in_local = jnp.einsum(
        "td,tc->dc", normed_all, d_projected, preferred_element_type=jnp.float32
    )
    step_spread = spread_two(d_step, low_block, high_block, heads_dev, head_total, 1)
    back_all = lax.psum_scatter(
        jnp.concatenate(
            [
                jnp.einsum("tc,dc->td", d_projected, in_local, preferred_element_type=jnp.float32),
                d_state,
                step_spread,
            ],
            axis=1,
        ),
        "col",
        scatter_dimension=0,
        tiled=True,
    )
    d_normed_in = back_all[:, :model]
    small_back = back_all[:, model:].astype(jnp.bfloat16)
    d_normed_in = d_normed_in + jnp.einsum(
        "tc,dc->td", small_back, small_full, preferred_element_type=jnp.float32
    )
    grad_small_part = jnp.einsum(
        "td,tc->dc", normed_in, small_back, preferred_element_type=jnp.float32
    )
    parts = grad_in_local.reshape((2,) * nd + (in_rows, rows, in_cols))
    parts = parts.transpose(tuple(range(nd - 1, -1, -1)) + (nd + 1, nd, nd + 2))
    grad_input = scatter_bits(parts, dp_steps + row_steps)
    scaled_in = d_normed_in * norm_gain[None, :]
    norm_part = jnp.sum(d_normed_in * x_float * inv_rms, axis=0)
    input_grad = (
        out_grad.astype(jnp.float32)
        + inv_rms * scaled_in
        - x_float * inv_rms**3 * jnp.mean(scaled_in * x_float, axis=1, keepdims=True)
    )
    gated_spread = spread_two(gain_part, low_block, high_block, inner_dev, inner, 0)
    conv_front = spread_two(d_conv_inner, low_block, high_block, inner_dev, inner, 1)
    conv_spread = jnp.concatenate([conv_front, d_conv_state], axis=1)
    coef_spread = spread_two(d_coefs, low_block, high_block, heads_dev, head_total, 1)
    pieces = (norm_part, gated_spread, conv_spread, coef_spread)
    offsets = [0]
    for piece in pieces:
        offsets.append(offsets[-1] + piece.size)
    packed = pack_rows(jnp.concatenate([piece.reshape(-1) for piece in pieces]), n_small)
    summed_flat = sum_bits(packed, all_steps).reshape(-1)
    grad_small = scatter_bits(split_blocks(grad_small_part, 0, all_axes, all_steps), all_steps)
    grad_norm, grad_gated, grad_conv, grad_coef = (
        summed_flat[offsets[k] : offsets[k + 1]].reshape(piece.shape)
        for k, piece in enumerate(pieces)
    )
    grad_state = grad_small[:, :n_state]
    grad_step = grad_small[:, n_state:]
    n_norm, f_norm, s_norm = adamw(
        norm_gain, grad_norm, first_norm_gain, second_norm_gain, VECTOR_RATE, 0.0
    )
    n_input, f_input, s_input = adamw(
        input_proj, grad_input, first_input_proj, second_input_proj, MATRIX_RATE, WEIGHT_DECAY
    )
    n_state, f_state, s_state = adamw(
        state_proj, grad_state, first_state_proj, second_state_proj, MATRIX_RATE, WEIGHT_DECAY
    )
    n_step, f_step, s_step = adamw(
        step_proj, grad_step, first_step_proj, second_step_proj, MATRIX_RATE, WEIGHT_DECAY
    )
    n_conv, f_conv, s_conv = adamw(
        conv_taps, grad_conv, first_conv_taps, second_conv_taps, VECTOR_RATE, 0.0
    )
    n_head, f_head, s_head = adamw(
        head_coef, grad_coef, first_head_coef, second_head_coef, VECTOR_RATE, 0.0
    )
    n_gated, f_gated, s_gated = adamw(
        gated_gain, grad_gated, first_gated_gain, second_gated_gain, VECTOR_RATE, 0.0
    )
    n_output, f_output, s_output = adamw(
        output_proj, grad_output, first_output_proj, second_output_proj, MATRIX_RATE, WEIGHT_DECAY
    )
    return (
        block_out,
        input_grad,
        grad_norm,
        grad_input,
        grad_state,
        grad_step,
        grad_conv,
        grad_coef,
        grad_gated,
        grad_output,
        n_norm,
        f_norm,
        s_norm,
        n_input,
        f_input,
        s_input,
        n_state,
        f_state,
        s_state,
        n_step,
        f_step,
        s_step,
        n_conv,
        f_conv,
        s_conv,
        n_head,
        f_head,
        s_head,
        n_gated,
        f_gated,
        s_gated,
        n_output,
        f_output,
        s_output,
    )


def solution(mesh):
    return jax.shard_map(
        per_device,
        mesh=mesh,
        in_specs=(
            P(("dp", "row", "col"), None),
            P(("dp", "row", "col"), None),
            P(),
            P(),
            P(),
            P("dp", ("row", "col")),
            P("dp", ("row", "col")),
            P("dp", ("row", "col")),
            P(("dp", "row", "col"), None),
            P(("dp", "row", "col"), None),
            P(("dp", "row", "col"), None),
            P(("dp", "row", "col"), None),
            P(("dp", "row", "col"), None),
            P(("dp", "row", "col"), None),
            P(),
            P(),
            P(),
            P(),
            P(),
            P(),
            P(),
            P(),
            P(),
            P(("row", "col"), "dp"),
            P(("row", "col"), "dp"),
            P(("row", "col"), "dp"),
        ),
        out_specs=(
            P(("dp", "row", "col"), None),
            P(("dp", "row", "col"), None),
            P(),
            P("dp", ("row", "col")),
            P(("dp", "row", "col"), None),
            P(("dp", "row", "col"), None),
            P(),
            P(),
            P(),
            P(("row", "col"), "dp"),
            P(),
            P(),
            P(),
            P("dp", ("row", "col")),
            P("dp", ("row", "col")),
            P("dp", ("row", "col")),
            P(("dp", "row", "col"), None),
            P(("dp", "row", "col"), None),
            P(("dp", "row", "col"), None),
            P(("dp", "row", "col"), None),
            P(("dp", "row", "col"), None),
            P(("dp", "row", "col"), None),
            P(),
            P(),
            P(),
            P(),
            P(),
            P(),
            P(),
            P(),
            P(),
            P(("row", "col"), "dp"),
            P(("row", "col"), "dp"),
            P(("row", "col"), "dp"),
        ),
        check_vma=False,
    )
```

```python
import jax
import jax.numpy as jnp
from jax import lax
from jax.sharding import PartitionSpec as P


SPAN = 256
SEQ_LEN = 1024
ADAM_STEP = 4


PRECISE = lax.Precision.HIGHEST
NORM_EPS = 1e-05
BETA_ONE = 0.9
BETA_TWO = 0.95
ADAM_EPS = 1e-08
MATRIX_RATE = 0.003
VECTOR_RATE = 0.1
WEIGHT_DECAY = 0.1


def causal_conv(values, filters):
    length = values.shape[0]
    padded = jnp.pad(values, ((3, 0), (0, 0)))
    summed = filters[4][None, :] + jnp.zeros_like(values)
    for offset in range(4):
        summed = summed + filters[offset][None, :] * padded[offset : offset + length]
    return summed


def span_scan(values, deltas, rates, key_rows, query_rows):
    length, head_count, head_width = values.shape
    states = key_rows.shape[1]
    blocks = length // SPAN
    values = values.reshape(blocks, SPAN, head_count, head_width)
    deltas = deltas.reshape(blocks, SPAN, head_count)
    key_rows = key_rows.reshape(blocks, SPAN, states)
    query_rows = query_rows.reshape(blocks, SPAN, states)
    lower = (jnp.arange(SPAN)[:, None] >= jnp.arange(SPAN)[None, :]).astype(jnp.float32)
    log_decay = jnp.einsum("qr,krh->kqh", lower, deltas * rates[None, None, :], precision=PRECISE)
    scores = jnp.einsum("kqn,krn->kqr", query_rows, key_rows, precision=PRECISE)
    causal = jnp.arange(SPAN)[:, None] >= jnp.arange(SPAN)[None, :]
    head_decay = jnp.transpose(log_decay, (0, 2, 1))
    head_deltas = jnp.transpose(deltas, (0, 2, 1))
    spread = head_decay[:, :, :, None] - head_decay[:, :, None, :]
    decays = jnp.exp(jnp.where(causal[None, None, :, :], spread, -jnp.inf))
    mixing = scores[:, None, :, :] * decays * head_deltas[:, :, None, :]
    within = jnp.einsum("khqr,krhp->kqhp", mixing, values, precision=PRECISE)
    to_end = jnp.exp(log_decay[:, -1:, :] - log_decay) * deltas
    produced = jnp.einsum("kqn,kqh,kqhp->khnp", key_rows, to_end, values, precision=PRECISE)
    factors = jnp.exp(log_decay[:, -1, :])
    carried = jnp.zeros((head_count, states, head_width), jnp.float32)
    entering = []
    for number in range(blocks):
        entering.append(carried)
        carried = carried * factors[number][:, None, None] + produced[number]
    entering = jnp.stack(entering)
    across = (
        jnp.einsum("kqn,khnp->kqhp", query_rows, entering, precision=PRECISE)
        * jnp.exp(log_decay)[:, :, :, None]
    )
    return (within + across).reshape(length, head_count, head_width)


def mixer_sequence(gate_part, inputs, state_in, step_raw, conv_inner, conv_state, coefs):
    length = inputs.shape[0]
    head_count = coefs.shape[1]
    head_width = inputs.shape[1] // head_count
    state_size = state_in.shape[1] // 2
    conv_out = jax.nn.silu(causal_conv(inputs, conv_inner))
    state_out = jax.nn.silu(causal_conv(state_in, conv_state))
    deltas = jax.nn.softplus(step_raw + coefs[0][None, :])
    rates = -jnp.exp(coefs[1])
    shaped = conv_out.reshape(length, head_count, head_width)
    result = span_scan(shaped, deltas, rates, state_out[:, :state_size], state_out[:, state_size:])
    result = result + coefs[2][None, :, None] * shaped
    return result.reshape(length, head_count * head_width) * jax.nn.silu(gate_part)


def mixer_all(gate_part, inputs, state_in, step_raw, conv_inner, conv_state, coefs):
    seq_count = inputs.shape[0] // SEQ_LEN

    def sequence(pieces):
        return mixer_sequence(
            pieces[0], pieces[1], pieces[2], pieces[3], conv_inner, conv_state, coefs
        )

    gated = lax.map(
        jax.checkpoint(sequence),
        (
            gate_part.reshape(seq_count, SEQ_LEN, -1),
            inputs.reshape(seq_count, SEQ_LEN, -1),
            state_in.reshape(seq_count, SEQ_LEN, -1),
            step_raw.reshape(seq_count, SEQ_LEN, -1),
        ),
    )
    return gated.reshape(inputs.shape[0], -1)


def adamw(weight, gradient, moment_one, moment_two, step_rate, shrink):
    new_one = BETA_ONE * moment_one + (1.0 - BETA_ONE) * gradient
    new_two = BETA_TWO * moment_two + (1.0 - BETA_TWO) * gradient * gradient
    one_hat = new_one / (1.0 - BETA_ONE**ADAM_STEP)
    two_hat = new_two / (1.0 - BETA_TWO**ADAM_STEP)
    updated = weight - step_rate * (one_hat / (jnp.sqrt(two_hat) + ADAM_EPS) + shrink * weight)
    return (updated, new_one, new_two)


def axis_bits(axis):
    return lax.axis_size(axis).bit_length() - 1


def bit_steps(*axes):
    return [(axis, k) for axis in axes for k in range(axis_bits(axis))]


def flip(x, axis, k):
    size = lax.axis_size(axis)
    return lax.ppermute(x, axis, [(j, j ^ (1 << k)) for j in range(size)])


def own_bit(axis, k):
    return (lax.axis_index(axis) >> k) & 1


def sum_bits(x, steps):
    for axis, k in steps:
        x = x + flip(x, axis, k)
    return x


def scatter_bits(x, steps):
    for axis, k in steps:
        b = own_bit(axis, k)
        keep = lax.dynamic_index_in_dim(x, b, 0, keepdims=False)
        send = lax.dynamic_index_in_dim(x, 1 - b, 0, keepdims=False)
        x = keep + flip(send, axis, k)
    return x


def gather_bits(x, steps):
    for axis, k in steps:
        other = flip(x, axis, k)
        x = jnp.where(own_bit(axis, k) == 0, jnp.stack([x, other]), jnp.stack([other, x]))
    return x


def gather_into(x, steps, names, target):
    names = list(names)
    for axis, k in steps:
        label = f"{axis}{k}"
        pos = sum(1 for n in names if target.index(n) < target.index(label))
        other = flip(x, axis, k)
        x = jnp.where(
            own_bit(axis, k) == 0,
            jnp.stack([x, other], axis=pos),
            jnp.stack([other, x], axis=pos),
        )
        names.insert(pos, label)
    return x


def bit_position(axes, step):
    axis, k = step
    below = sum(axis_bits(a) for a in axes[axes.index(axis) + 1 :])
    return below + k


def split_blocks(x, dim, axes, steps):
    total = sum(axis_bits(a) for a in axes)
    shape = x.shape[:dim] + (2,) * total + (x.shape[dim] >> total,) + x.shape[dim + 1 :]
    x = x.reshape(shape)
    front = [dim + total - 1 - bit_position(axes, s) for s in steps]
    rest = [j for j in range(len(shape)) if j not in front]
    return x.transpose(front + rest)


def pack_rows(values, width):
    flat = values.reshape(-1)
    rows = -(-flat.shape[0] // width)
    return jnp.pad(flat, (0, rows * width - flat.shape[0])).reshape(rows, width)


def two_blocks(values, first, second, width, axis):
    return jnp.concatenate(
        [
            lax.dynamic_slice_in_dim(values, first * width, width, axis),
            lax.dynamic_slice_in_dim(values, second * width, width, axis),
        ],
        axis=axis,
    )


def spread_two(values, first, second, width, total, axis):
    reps = [1] * values.ndim
    reps[axis] = total // width
    block = (jnp.arange(total) // width).reshape([-1 if k == axis else 1 for k in range(values.ndim)])
    low = jnp.tile(lax.slice_in_dim(values, 0, width, axis=axis), reps)
    high = jnp.tile(lax.slice_in_dim(values, width, 2 * width, axis=axis), reps)
    return jnp.where(block == first, low, jnp.where(block == second, high, 0.0))


def per_device(
    block_in,
    out_grad,
    norm_gain,
    first_norm_gain,
    second_norm_gain,
    input_proj,
    first_input_proj,
    second_input_proj,
    state_proj,
    first_state_proj,
    second_state_proj,
    step_proj,
    first_step_proj,
    second_step_proj,
    conv_taps,
    first_conv_taps,
    second_conv_taps,
    head_coef,
    first_head_coef,
    second_head_coef,
    gated_gain,
    first_gated_gain,
    second_gated_gain,
    output_proj,
    first_output_proj,
    second_output_proj,
):
    groups = lax.axis_size(("row", "col"))
    cols = lax.axis_size("col")
    rows = lax.axis_size("row")
    col = lax.axis_index("col")
    tok_dev = block_in.shape[0]
    model = block_in.shape[1]
    seq_tok = tok_dev * cols
    inner = gated_gain.shape[0]
    inner_dev = inner // groups
    head_total = head_coef.shape[1]
    heads_dev = head_total // groups
    head_width = inner // head_total
    n_state = state_proj.shape[1]
    n_small = n_state + step_proj.shape[1]
    rows_dev = state_proj.shape[0]
    in_rows, in_cols = input_proj.shape
    out_rows, out_cols = output_proj.shape
    low_block = col
    high_block = col + cols * (rows - 1)
    all_axes = ("dp", "row", "col")
    all_steps = bit_steps(*all_axes)
    dp_steps = bit_steps("dp")
    row_steps = bit_steps("row")
    col_steps = bit_steps("col")
    nd = len(dp_steps)
    small = jnp.concatenate([state_proj, step_proj], axis=1).astype(jnp.bfloat16)
    gather_steps = [("dp", k) for k in range(nd - 1, 0, -1)] + row_steps + [("dp", 0)]
    dp_names = [f"dp{k}" for k in range(nd - 1, -1, -1)]
    in_g = gather_into(
        input_proj.astype(jnp.bfloat16),
        gather_steps,
        ["i", "j"],
        ["row0"] + dp_names + ["i", "j"],
    ).reshape(rows, (1 << nd) * in_rows, in_cols)
    out_g = gather_into(
        output_proj.astype(jnp.bfloat16),
        gather_steps,
        ["i", "j"],
        dp_names + ["row0", "i", "j"],
    ).reshape(1 << nd, rows, out_rows, out_cols)
    x_float = block_in.astype(jnp.float32)
    inv_rms = lax.rsqrt(jnp.mean(x_float * x_float, axis=1, keepdims=True) + NORM_EPS)
    normed_in = (x_float * inv_rms * norm_gain[None, :]).astype(jnp.bfloat16)
    tokens = lax.all_gather(
        jnp.concatenate([normed_in, pack_rows(small, model)], axis=0), "col", axis=0
    )
    normed_all = tokens[:, :tok_dev].reshape(seq_tok, model)
    small_col = tokens[:, tok_dev:].reshape(cols, -1)[:, : rows_dev * n_small].reshape(-1, n_small)
    small_full = gather_bits(small_col, row_steps + dp_steps).reshape(-1, n_small)
    cotangent = lax.all_gather(out_grad, "col", axis=0, tiled=True)
    projected = jnp.einsum(
        "tD,rDj->trj", normed_all, in_g, preferred_element_type=jnp.float32
    ).reshape(seq_tok, rows * in_cols)
    small_all = jnp.dot(normed_all, small_full, preferred_element_type=jnp.float32).astype(
        jnp.bfloat16
    )
    state_all = small_all[:, :n_state]
    step_all = small_all[:, n_state:]
    local_heads = 2 * heads_dev
    local_inner = 2 * inner_dev
    paired = projected.reshape(seq_tok, local_heads, 2, head_width)
    gate_part = paired[:, :, 0, :].reshape(seq_tok, local_inner)
    inputs = paired[:, :, 1, :].reshape(seq_tok, local_inner)
    conv_inner = two_blocks(conv_taps[:, :inner], low_block, high_block, inner_dev, 1)
    conv_state = conv_taps[:, inner:]
    coefs = two_blocks(head_coef, low_block, high_block, heads_dev, 1)
    step_local = two_blocks(step_all, low_block, high_block, heads_dev, 1).astype(jnp.float32)
    gated, mixer_pull = jax.vjp(
        mixer_all,
        gate_part,
        inputs,
        state_all.astype(jnp.float32),
        step_local,
        conv_inner,
        conv_state,
        coefs,
    )
    squares = sum_bits(jnp.sum(gated * gated, axis=1), col_steps)
    gated_rms = lax.rsqrt(squares / inner + NORM_EPS)[:, None]
    gain_local = two_blocks(gated_gain, low_block, high_block, inner_dev, 0)
    normed_out = (gated * gated_rms * gain_local[None, :]).astype(jnp.bfloat16)
    mixed = lax.psum_scatter(
        jnp.einsum(
            "tri,drij->tdj",
            normed_out.reshape(seq_tok, rows, out_rows),
            out_g,
            preferred_element_type=jnp.float32,
        ).reshape(seq_tok, model),
        "col",
        scatter_dimension=0,
        tiled=True,
    )
    block_out = (x_float + mixed).astype(jnp.bfloat16)
    grad_out_local = jnp.einsum(
        "tc,td->cd", normed_out, cotangent, preferred_element_type=jnp.float32
    )
    parts = grad_out_local.reshape((rows, out_rows) + (2,) * nd + (out_cols,))
    parts = parts.transpose(tuple(range(nd + 1, 1, -1)) + (0, 1, nd + 2))
    grad_output = scatter_bits(parts, dp_steps + row_steps)
    d_normed = jnp.einsum(
        "tdj,drij->tri",
        cotangent.reshape(seq_tok, 1 << nd, out_cols),
        out_g,
        preferred_element_type=jnp.float32,
    ).reshape(seq_tok, rows * out_rows)
    gain_part = jnp.sum(d_normed * gated * gated_rms, axis=0)
    scaled = d_normed * gain_local[None, :]
    cross = sum_bits(jnp.sum(scaled * gated, axis=1), col_steps)
    d_gated = gated_rms * scaled - gated * gated_rms**3 * (cross / inner)[:, None]
    d_gate, d_inputs, d_state, d_step, d_conv_inner, d_conv_state, d_coefs = mixer_pull(
        d_gated
    )
    d_projected = (
        jnp.stack(
            [
                d_gate.reshape(seq_tok, local_heads, head_width),
                d_inputs.reshape(seq_tok, local_heads, head_width),
            ],
            axis=2,
        )
        .reshape(seq_tok, 2 * local_inner)
        .astype(jnp.bfloat16)
    )
    grad_in_local = jnp.einsum(
        "td,tc->dc", normed_all, d_projected, preferred_element_type=jnp.float32
    )
    step_spread = spread_two(d_step, low_block, high_block, heads_dev, head_total, 1)
    back_all = lax.psum_scatter(
        jnp.concatenate(
            [
                jnp.einsum(
                    "trj,rDj->tD",
                    d_projected.reshape(seq_tok, rows, in_cols),
                    in_g,
                    preferred_element_type=jnp.float32,
                ),
                d_state,
                step_spread,
            ],
            axis=1,
        ),
        "col",
        scatter_dimension=0,
        tiled=True,
    )
    d_normed_in = back_all[:, :model]
    small_back = back_all[:, model:].astype(jnp.bfloat16)
    d_normed_in = d_normed_in + jnp.einsum(
        "tc,dc->td", small_back, small_full, preferred_element_type=jnp.float32
    )
    grad_small_part = jnp.einsum(
        "td,tc->dc", normed_in, small_back, preferred_element_type=jnp.float32
    )
    parts = grad_in_local.reshape((2,) * nd + (in_rows, rows, in_cols))
    parts = parts.transpose(tuple(range(nd - 1, -1, -1)) + (nd + 1, nd, nd + 2))
    half = in_cols // 2
    first_half = scatter_bits(parts[..., :half], dp_steps + row_steps)
    swapped = jnp.moveaxis(parts[..., half:], nd, 1)
    second_half = scatter_bits(swapped, dp_steps[:1] + row_steps + dp_steps[1:])
    grad_input = jnp.concatenate([first_half, second_half], axis=1)
    scaled_in = d_normed_in * norm_gain[None, :]
    norm_part = jnp.sum(d_normed_in * x_float * inv_rms, axis=0)
    input_grad = (
        out_grad.astype(jnp.float32)
        + inv_rms * scaled_in
        - x_float * inv_rms**3 * jnp.mean(scaled_in * x_float, axis=1, keepdims=True)
    )
    gated_spread = spread_two(gain_part, low_block, high_block, inner_dev, inner, 0)
    conv_front = spread_two(d_conv_inner, low_block, high_block, inner_dev, inner, 1)
    conv_spread = jnp.concatenate([conv_front, d_conv_state], axis=1)
    coef_spread = spread_two(d_coefs, low_block, high_block, heads_dev, head_total, 1)
    pieces = (norm_part, gated_spread, conv_spread, coef_spread)
    offsets = [0]
    for piece in pieces:
        offsets.append(offsets[-1] + piece.size)
    packed = pack_rows(jnp.concatenate([piece.reshape(-1) for piece in pieces]), n_small)
    summed_flat = sum_bits(packed, all_steps).reshape(-1)
    grad_small = scatter_bits(split_blocks(grad_small_part, 0, all_axes, all_steps), all_steps)
    grad_norm, grad_gated, grad_conv, grad_coef = (
        summed_flat[offsets[k] : offsets[k + 1]].reshape(piece.shape)
        for k, piece in enumerate(pieces)
    )
    grad_state = grad_small[:, :n_state]
    grad_step = grad_small[:, n_state:]
    n_norm, f_norm, s_norm = adamw(
        norm_gain, grad_norm, first_norm_gain, second_norm_gain, VECTOR_RATE, 0.0
    )
    n_input, f_input, s_input = adamw(
        input_proj, grad_input, first_input_proj, second_input_proj, MATRIX_RATE, WEIGHT_DECAY
    )
    n_state, f_state, s_state = adamw(
        state_proj, grad_state, first_state_proj, second_state_proj, MATRIX_RATE, WEIGHT_DECAY
    )
    n_step, f_step, s_step = adamw(
        step_proj, grad_step, first_step_proj, second_step_proj, MATRIX_RATE, WEIGHT_DECAY
    )
    n_conv, f_conv, s_conv = adamw(
        conv_taps, grad_conv, first_conv_taps, second_conv_taps, VECTOR_RATE, 0.0
    )
    n_head, f_head, s_head = adamw(
        head_coef, grad_coef, first_head_coef, second_head_coef, VECTOR_RATE, 0.0
    )
    n_gated, f_gated, s_gated = adamw(
        gated_gain, grad_gated, first_gated_gain, second_gated_gain, VECTOR_RATE, 0.0
    )
    n_output, f_output, s_output = adamw(
        output_proj, grad_output, first_output_proj, second_output_proj, MATRIX_RATE, WEIGHT_DECAY
    )
    return (
        block_out,
        input_grad,
        grad_norm,
        grad_input,
        grad_state,
        grad_step,
        grad_conv,
        grad_coef,
        grad_gated,
        grad_output,
        n_norm,
        f_norm,
        s_norm,
        n_input,
        f_input,
        s_input,
        n_state,
        f_state,
        s_state,
        n_step,
        f_step,
        s_step,
        n_conv,
        f_conv,
        s_conv,
        n_head,
        f_head,
        s_head,
        n_gated,
        f_gated,
        s_gated,
        n_output,
        f_output,
        s_output,
    )


def solution(mesh):
    return jax.shard_map(
        per_device,
        mesh=mesh,
        in_specs=(
            P(("dp", "row", "col"), None),
            P(("dp", "row", "col"), None),
            P(),
            P(),
            P(),
            P("dp", ("row", "col")),
            P("dp", ("row", "col")),
            P("dp", ("row", "col")),
            P(("dp", "row", "col"), None),
            P(("dp", "row", "col"), None),
            P(("dp", "row", "col"), None),
            P(("dp", "row", "col"), None),
            P(("dp", "row", "col"), None),
            P(("dp", "row", "col"), None),
            P(),
            P(),
            P(),
            P(),
            P(),
            P(),
            P(),
            P(),
            P(),
            P(("row", "col"), "dp"),
            P(("row", "col"), "dp"),
            P(("row", "col"), "dp"),
        ),
        out_specs=(
            P(("dp", "row", "col"), None),
            P(("dp", "row", "col"), None),
            P(),
            P("dp", ("row", "col")),
            P(("dp", "row", "col"), None),
            P(("dp", "row", "col"), None),
            P(),
            P(),
            P(),
            P(("row", "col"), "dp"),
            P(),
            P(),
            P(),
            P("dp", ("row", "col")),
            P("dp", ("row", "col")),
            P("dp", ("row", "col")),
            P(("dp", "row", "col"), None),
            P(("dp", "row", "col"), None),
            P(("dp", "row", "col"), None),
            P(("dp", "row", "col"), None),
            P(("dp", "row", "col"), None),
            P(("dp", "row", "col"), None),
            P(),
            P(),
            P(),
            P(),
            P(),
            P(),
            P(),
            P(),
            P(),
            P(("row", "col"), "dp"),
            P(("row", "col"), "dp"),
            P(("row", "col"), "dp"),
        ),
        check_vma=False,
    )
```

```python
import jax
import jax.numpy as jnp
from jax import lax
from jax.sharding import PartitionSpec as P


SPAN = 256
SEQ_LEN = 1024
ADAM_STEP = 4


PRECISE = lax.Precision.HIGHEST
SCAN_PRECISION = lax.Precision.HIGH
NORM_EPS = 1e-05
BETA_ONE = 0.9
BETA_TWO = 0.95
ADAM_EPS = 1e-08
MATRIX_RATE = 0.003
VECTOR_RATE = 0.1
WEIGHT_DECAY = 0.1


def causal_conv(values, filters):
    length = values.shape[0]
    padded = jnp.pad(values, ((3, 0), (0, 0)))
    summed = filters[4][None, :] + jnp.zeros_like(values)
    for offset in range(4):
        summed = summed + filters[offset][None, :] * padded[offset : offset + length]
    return summed


def span_scan(values, deltas, rates, key_rows, query_rows):
    length, head_count, head_width = values.shape
    states = key_rows.shape[1]
    blocks = length // SPAN
    values = values.reshape(blocks, SPAN, head_count, head_width)
    deltas = deltas.reshape(blocks, SPAN, head_count)
    key_rows = key_rows.reshape(blocks, SPAN, states)
    query_rows = query_rows.reshape(blocks, SPAN, states)
    lower = (jnp.arange(SPAN)[:, None] >= jnp.arange(SPAN)[None, :]).astype(jnp.float32)
    log_decay = jnp.einsum("qr,krh->kqh", lower, deltas * rates[None, None, :], precision=PRECISE)
    scores = jnp.einsum("kqn,krn->kqr", query_rows, key_rows, precision=SCAN_PRECISION)
    causal = jnp.arange(SPAN)[:, None] >= jnp.arange(SPAN)[None, :]
    head_decay = jnp.transpose(log_decay, (0, 2, 1))
    head_deltas = jnp.transpose(deltas, (0, 2, 1))
    spread = head_decay[:, :, :, None] - head_decay[:, :, None, :]
    decays = jnp.exp(jnp.where(causal[None, None, :, :], spread, -jnp.inf))
    mixing = scores[:, None, :, :] * decays * head_deltas[:, :, None, :]
    within = jnp.einsum("khqr,krhp->kqhp", mixing, values, precision=SCAN_PRECISION)
    to_end = jnp.exp(log_decay[:, -1:, :] - log_decay) * deltas
    produced = jnp.einsum(
        "kqn,kqh,kqhp->khnp", key_rows, to_end, values, precision=SCAN_PRECISION
    )
    factors = jnp.exp(log_decay[:, -1, :])
    carried = jnp.zeros((head_count, states, head_width), jnp.float32)
    entering = []
    for number in range(blocks):
        entering.append(carried)
        carried = carried * factors[number][:, None, None] + produced[number]
    entering = jnp.stack(entering)
    across = (
        jnp.einsum("kqn,khnp->kqhp", query_rows, entering, precision=SCAN_PRECISION)
        * jnp.exp(log_decay)[:, :, :, None]
    )
    return (within + across).reshape(length, head_count, head_width)


def mixer_sequence(gate_part, inputs, state_in, step_raw, conv_inner, conv_state, coefs):
    length = inputs.shape[0]
    head_count = coefs.shape[1]
    head_width = inputs.shape[1] // head_count
    state_size = state_in.shape[1] // 2
    conv_out = jax.nn.silu(causal_conv(inputs, conv_inner))
    state_out = jax.nn.silu(causal_conv(state_in, conv_state))
    deltas = jax.nn.softplus(step_raw + coefs[0][None, :])
    rates = -jnp.exp(coefs[1])
    shaped = conv_out.reshape(length, head_count, head_width)
    result = span_scan(shaped, deltas, rates, state_out[:, :state_size], state_out[:, state_size:])
    result = result + coefs[2][None, :, None] * shaped
    return result.reshape(length, head_count * head_width) * jax.nn.silu(gate_part)


def mixer_all(gate_part, inputs, state_in, step_raw, conv_inner, conv_state, coefs):
    seq_count = inputs.shape[0] // SEQ_LEN

    def sequence(pieces):
        return mixer_sequence(
            pieces[0], pieces[1], pieces[2], pieces[3], conv_inner, conv_state, coefs
        )

    gated = lax.map(
        jax.checkpoint(sequence),
        (
            gate_part.reshape(seq_count, SEQ_LEN, -1),
            inputs.reshape(seq_count, SEQ_LEN, -1),
            state_in.reshape(seq_count, SEQ_LEN, -1),
            step_raw.reshape(seq_count, SEQ_LEN, -1),
        ),
    )
    return gated.reshape(inputs.shape[0], -1)


def adamw(weight, gradient, moment_one, moment_two, step_rate, shrink):
    new_one = BETA_ONE * moment_one + (1.0 - BETA_ONE) * gradient
    new_two = BETA_TWO * moment_two + (1.0 - BETA_TWO) * gradient * gradient
    one_hat = new_one / (1.0 - BETA_ONE**ADAM_STEP)
    two_hat = new_two / (1.0 - BETA_TWO**ADAM_STEP)
    updated = weight - step_rate * (one_hat / (jnp.sqrt(two_hat) + ADAM_EPS) + shrink * weight)
    return (updated, new_one, new_two)


def axis_bits(axis):
    return lax.axis_size(axis).bit_length() - 1


def bit_steps(*axes):
    return [(axis, k) for axis in axes for k in range(axis_bits(axis))]


def flip(x, axis, k):
    size = lax.axis_size(axis)
    return lax.ppermute(x, axis, [(j, j ^ (1 << k)) for j in range(size)])


def own_bit(axis, k):
    return (lax.axis_index(axis) >> k) & 1


def sum_bits(x, steps):
    for axis, k in steps:
        x = x + flip(x, axis, k)
    return x


def scatter_bits(x, steps):
    for axis, k in steps:
        b = own_bit(axis, k)
        keep = lax.dynamic_index_in_dim(x, b, 0, keepdims=False)
        send = lax.dynamic_index_in_dim(x, 1 - b, 0, keepdims=False)
        x = keep + flip(send, axis, k)
    return x


def scatter_sum_bits(x, extra, steps):
    for axis, k in steps:
        b = own_bit(axis, k)
        keep = lax.dynamic_index_in_dim(x, b, 0, keepdims=False)
        send = lax.dynamic_index_in_dim(x, 1 - b, 0, keepdims=False)
        flat = send.reshape(-1, extra.shape[1])
        got = flip(jnp.concatenate([flat, extra], axis=0), axis, k)
        x = keep + got[: flat.shape[0]].reshape(send.shape)
        extra = extra + got[flat.shape[0] :]
    return x, extra


def gather_bits(x, steps):
    for axis, k in steps:
        other = flip(x, axis, k)
        x = jnp.where(own_bit(axis, k) == 0, jnp.stack([x, other]), jnp.stack([other, x]))
    return x


def gather_into(x, steps, names, target):
    names = list(names)
    for axis, k in steps:
        label = f"{axis}{k}"
        pos = sum(1 for n in names if target.index(n) < target.index(label))
        other = flip(x, axis, k)
        x = jnp.where(
            own_bit(axis, k) == 0,
            jnp.stack([x, other], axis=pos),
            jnp.stack([other, x], axis=pos),
        )
        names.insert(pos, label)
    return x


def bit_position(axes, step):
    axis, k = step
    below = sum(axis_bits(a) for a in axes[axes.index(axis) + 1 :])
    return below + k


def split_blocks(x, dim, axes, steps):
    total = sum(axis_bits(a) for a in axes)
    shape = x.shape[:dim] + (2,) * total + (x.shape[dim] >> total,) + x.shape[dim + 1 :]
    x = x.reshape(shape)
    front = [dim + total - 1 - bit_position(axes, s) for s in steps]
    rest = [j for j in range(len(shape)) if j not in front]
    return x.transpose(front + rest)


def pack_rows(values, width):
    flat = values.reshape(-1)
    rows = -(-flat.shape[0] // width)
    return jnp.pad(flat, (0, rows * width - flat.shape[0])).reshape(rows, width)


def two_blocks(values, first, second, width, axis):
    return jnp.concatenate(
        [
            lax.dynamic_slice_in_dim(values, first * width, width, axis),
            lax.dynamic_slice_in_dim(values, second * width, width, axis),
        ],
        axis=axis,
    )


def spread_two(values, first, second, width, total, axis):
    reps = [1] * values.ndim
    reps[axis] = total // width
    block = (jnp.arange(total) // width).reshape([-1 if k == axis else 1 for k in range(values.ndim)])
    low = jnp.tile(lax.slice_in_dim(values, 0, width, axis=axis), reps)
    high = jnp.tile(lax.slice_in_dim(values, width, 2 * width, axis=axis), reps)
    return jnp.where(block == first, low, jnp.where(block == second, high, 0.0))


def per_device(
    block_in,
    out_grad,
    norm_gain,
    first_norm_gain,
    second_norm_gain,
    input_proj,
    first_input_proj,
    second_input_proj,
    state_proj,
    first_state_proj,
    second_state_proj,
    step_proj,
    first_step_proj,
    second_step_proj,
    conv_taps,
    first_conv_taps,
    second_conv_taps,
    head_coef,
    first_head_coef,
    second_head_coef,
    gated_gain,
    first_gated_gain,
    second_gated_gain,
    output_proj,
    first_output_proj,
    second_output_proj,
):
    groups = lax.axis_size(("row", "col"))
    cols = lax.axis_size("col")
    rows = lax.axis_size("row")
    col = lax.axis_index("col")
    tok_dev = block_in.shape[0]
    model = block_in.shape[1]
    seq_tok = tok_dev * cols
    inner = gated_gain.shape[0]
    inner_dev = inner // groups
    head_total = head_coef.shape[1]
    heads_dev = head_total // groups
    head_width = inner // head_total
    n_state = state_proj.shape[1]
    n_small = n_state + step_proj.shape[1]
    rows_dev = state_proj.shape[0]
    in_rows, in_cols = input_proj.shape
    out_rows, out_cols = output_proj.shape
    low_block = col
    high_block = col + cols * (rows - 1)
    all_axes = ("dp", "row", "col")
    all_steps = bit_steps(*all_axes)
    dp_steps = bit_steps("dp")
    row_steps = bit_steps("row")
    col_steps = bit_steps("col")
    nd = len(dp_steps)
    small = jnp.concatenate([state_proj, step_proj], axis=1).astype(jnp.bfloat16)
    gather_steps = [("dp", k) for k in range(nd - 1, 0, -1)] + row_steps + [("dp", 0)]
    dp_names = [f"dp{k}" for k in range(nd - 1, -1, -1)]
    in_g = gather_into(
        input_proj.astype(jnp.bfloat16),
        gather_steps,
        ["i", "j"],
        ["row0"] + dp_names + ["i", "j"],
    ).reshape(rows, (1 << nd) * in_rows, in_cols)
    out_g = gather_into(
        output_proj.astype(jnp.bfloat16),
        gather_steps,
        ["i", "j"],
        dp_names + ["row0", "i", "j"],
    ).reshape(1 << nd, rows, out_rows, out_cols)
    x_float = block_in.astype(jnp.float32)
    inv_rms = lax.rsqrt(jnp.mean(x_float * x_float, axis=1, keepdims=True) + NORM_EPS)
    normed_in = (x_float * inv_rms * norm_gain[None, :]).astype(jnp.bfloat16)
    tokens = lax.all_gather(
        jnp.concatenate([normed_in, pack_rows(small, model)], axis=0), "col", axis=0
    )
    normed_all = tokens[:, :tok_dev].reshape(seq_tok, model)
    small_col = tokens[:, tok_dev:].reshape(cols, -1)[:, : rows_dev * n_small].reshape(-1, n_small)
    small_full = gather_bits(small_col, row_steps + dp_steps).reshape(-1, n_small)
    cotangent = lax.all_gather(out_grad, "col", axis=0, tiled=True)
    projected = jnp.einsum(
        "tD,rDj->trj", normed_all, in_g, preferred_element_type=jnp.float32
    ).reshape(seq_tok, rows * in_cols)
    small_all = jnp.dot(normed_all, small_full, preferred_element_type=jnp.float32).astype(
        jnp.bfloat16
    )
    state_all = small_all[:, :n_state]
    step_all = small_all[:, n_state:]
    local_heads = 2 * heads_dev
    local_inner = 2 * inner_dev
    paired = projected.reshape(seq_tok, local_heads, 2, head_width)
    gate_part = paired[:, :, 0, :].reshape(seq_tok, local_inner)
    inputs = paired[:, :, 1, :].reshape(seq_tok, local_inner)
    conv_inner = two_blocks(conv_taps[:, :inner], low_block, high_block, inner_dev, 1)
    conv_state = conv_taps[:, inner:]
    coefs = two_blocks(head_coef, low_block, high_block, heads_dev, 1)
    step_local = two_blocks(step_all, low_block, high_block, heads_dev, 1).astype(jnp.float32)
    gated, mixer_pull = jax.vjp(
        mixer_all,
        gate_part,
        inputs,
        state_all.astype(jnp.float32),
        step_local,
        conv_inner,
        conv_state,
        coefs,
    )
    squares = sum_bits(jnp.sum(gated * gated, axis=1), col_steps)
    gated_rms = lax.rsqrt(squares / inner + NORM_EPS)[:, None]
    gain_local = two_blocks(gated_gain, low_block, high_block, inner_dev, 0)
    normed_out = (gated * gated_rms * gain_local[None, :]).astype(jnp.bfloat16)
    mixed = lax.psum_scatter(
        jnp.einsum(
            "tri,drij->tdj",
            normed_out.reshape(seq_tok, rows, out_rows),
            out_g,
            preferred_element_type=jnp.float32,
        ).reshape(seq_tok, model),
        "col",
        scatter_dimension=0,
        tiled=True,
    )
    block_out = (x_float + mixed).astype(jnp.bfloat16)
    grad_out_local = jnp.einsum(
        "tc,td->cd", normed_out, cotangent, preferred_element_type=jnp.float32
    )
    parts = grad_out_local.reshape((rows, out_rows) + (2,) * nd + (out_cols,))
    parts = parts.transpose(tuple(range(nd + 1, 1, -1)) + (0, 1, nd + 2))
    grad_output = scatter_bits(parts, dp_steps + row_steps)
    d_normed = jnp.einsum(
        "tdj,drij->tri",
        cotangent.reshape(seq_tok, 1 << nd, out_cols),
        out_g,
        preferred_element_type=jnp.float32,
    ).reshape(seq_tok, rows * out_rows)
    gain_part = jnp.sum(d_normed * gated * gated_rms, axis=0)
    scaled = d_normed * gain_local[None, :]
    cross = sum_bits(jnp.sum(scaled * gated, axis=1), col_steps)
    d_gated = gated_rms * scaled - gated * gated_rms**3 * (cross / inner)[:, None]
    d_gate, d_inputs, d_state, d_step, d_conv_inner, d_conv_state, d_coefs = mixer_pull(
        d_gated
    )
    d_projected = (
        jnp.stack(
            [
                d_gate.reshape(seq_tok, local_heads, head_width),
                d_inputs.reshape(seq_tok, local_heads, head_width),
            ],
            axis=2,
        )
        .reshape(seq_tok, 2 * local_inner)
        .astype(jnp.bfloat16)
    )
    grad_in_local = jnp.einsum(
        "td,tc->dc", normed_all, d_projected, preferred_element_type=jnp.float32
    )
    step_spread = spread_two(d_step, low_block, high_block, heads_dev, head_total, 1)
    back_all = lax.psum_scatter(
        jnp.concatenate(
            [
                jnp.einsum(
                    "trj,rDj->tD",
                    d_projected.reshape(seq_tok, rows, in_cols),
                    in_g,
                    preferred_element_type=jnp.float32,
                ),
                d_state,
                step_spread,
            ],
            axis=1,
        ),
        "col",
        scatter_dimension=0,
        tiled=True,
    )
    d_normed_in = back_all[:, :model]
    small_back = back_all[:, model:].astype(jnp.bfloat16)
    d_normed_in = d_normed_in + jnp.einsum(
        "tc,dc->td", small_back, small_full, preferred_element_type=jnp.float32
    )
    grad_small_part = jnp.einsum(
        "td,tc->dc", normed_in, small_back, preferred_element_type=jnp.float32
    )
    parts = grad_in_local.reshape((2,) * nd + (in_rows, rows, in_cols))
    parts = parts.transpose(tuple(range(nd - 1, -1, -1)) + (nd + 1, nd, nd + 2))
    half = in_cols // 2
    first_half = scatter_bits(parts[..., :half], dp_steps + row_steps)
    swapped = jnp.moveaxis(parts[..., half:], nd, 1)
    second_half = scatter_bits(swapped, dp_steps[:1] + row_steps + dp_steps[1:])
    grad_input = jnp.concatenate([first_half, second_half], axis=1)
    scaled_in = d_normed_in * norm_gain[None, :]
    norm_part = jnp.sum(d_normed_in * x_float * inv_rms, axis=0)
    input_grad = (
        out_grad.astype(jnp.float32)
        + inv_rms * scaled_in
        - x_float * inv_rms**3 * jnp.mean(scaled_in * x_float, axis=1, keepdims=True)
    )
    gated_spread = spread_two(gain_part, low_block, high_block, inner_dev, inner, 0)
    conv_front = spread_two(d_conv_inner, low_block, high_block, inner_dev, inner, 1)
    conv_spread = jnp.concatenate([conv_front, d_conv_state], axis=1)
    coef_spread = spread_two(d_coefs, low_block, high_block, heads_dev, head_total, 1)
    pieces = (gated_spread, conv_spread, coef_spread)
    offsets = [0]
    for piece in pieces:
        offsets.append(offsets[-1] + piece.size)
    packed = pack_rows(jnp.concatenate([piece.reshape(-1) for piece in pieces]), n_small)
    summed_flat = sum_bits(packed, all_steps).reshape(-1)
    grad_gated, grad_conv, grad_coef = (
        summed_flat[offsets[k] : offsets[k + 1]].reshape(piece.shape)
        for k, piece in enumerate(pieces)
    )
    grad_small, norm_summed = scatter_sum_bits(
        split_blocks(grad_small_part, 0, all_axes, all_steps),
        pack_rows(norm_part, n_small),
        all_steps,
    )
    grad_norm = norm_summed.reshape(-1)[: norm_part.shape[0]]
    grad_state = grad_small[:, :n_state]
    grad_step = grad_small[:, n_state:]
    n_norm, f_norm, s_norm = adamw(
        norm_gain, grad_norm, first_norm_gain, second_norm_gain, VECTOR_RATE, 0.0
    )
    n_input, f_input, s_input = adamw(
        input_proj, grad_input, first_input_proj, second_input_proj, MATRIX_RATE, WEIGHT_DECAY
    )
    n_state, f_state, s_state = adamw(
        state_proj, grad_state, first_state_proj, second_state_proj, MATRIX_RATE, WEIGHT_DECAY
    )
    n_step, f_step, s_step = adamw(
        step_proj, grad_step, first_step_proj, second_step_proj, MATRIX_RATE, WEIGHT_DECAY
    )
    n_conv, f_conv, s_conv = adamw(
        conv_taps, grad_conv, first_conv_taps, second_conv_taps, VECTOR_RATE, 0.0
    )
    n_head, f_head, s_head = adamw(
        head_coef, grad_coef, first_head_coef, second_head_coef, VECTOR_RATE, 0.0
    )
    n_gated, f_gated, s_gated = adamw(
        gated_gain, grad_gated, first_gated_gain, second_gated_gain, VECTOR_RATE, 0.0
    )
    n_output, f_output, s_output = adamw(
        output_proj, grad_output, first_output_proj, second_output_proj, MATRIX_RATE, WEIGHT_DECAY
    )
    return (
        block_out,
        input_grad,
        grad_norm,
        grad_input,
        grad_state,
        grad_step,
        grad_conv,
        grad_coef,
        grad_gated,
        grad_output,
        n_norm,
        f_norm,
        s_norm,
        n_input,
        f_input,
        s_input,
        n_state,
        f_state,
        s_state,
        n_step,
        f_step,
        s_step,
        n_conv,
        f_conv,
        s_conv,
        n_head,
        f_head,
        s_head,
        n_gated,
        f_gated,
        s_gated,
        n_output,
        f_output,
        s_output,
    )


def solution(mesh):
    return jax.shard_map(
        per_device,
        mesh=mesh,
        in_specs=(
            P(("dp", "row", "col"), None),
            P(("dp", "row", "col"), None),
            P(),
            P(),
            P(),
            P("dp", ("row", "col")),
            P("dp", ("row", "col")),
            P("dp", ("row", "col")),
            P(("dp", "row", "col"), None),
            P(("dp", "row", "col"), None),
            P(("dp", "row", "col"), None),
            P(("dp", "row", "col"), None),
            P(("dp", "row", "col"), None),
            P(("dp", "row", "col"), None),
            P(),
            P(),
            P(),
            P(),
            P(),
            P(),
            P(),
            P(),
            P(),
            P(("row", "col"), "dp"),
            P(("row", "col"), "dp"),
            P(("row", "col"), "dp"),
        ),
        out_specs=(
            P(("dp", "row", "col"), None),
            P(("dp", "row", "col"), None),
            P(),
            P("dp", ("row", "col")),
            P(("dp", "row", "col"), None),
            P(("dp", "row", "col"), None),
            P(),
            P(),
            P(),
            P(("row", "col"), "dp"),
            P(),
            P(),
            P(),
            P("dp", ("row", "col")),
            P("dp", ("row", "col")),
            P("dp", ("row", "col")),
            P(("dp", "row", "col"), None),
            P(("dp", "row", "col"), None),
            P(("dp", "row", "col"), None),
            P(("dp", "row", "col"), None),
            P(("dp", "row", "col"), None),
            P(("dp", "row", "col"), None),
            P(),
            P(),
            P(),
            P(),
            P(),
            P(),
            P(),
            P(),
            P(),
            P(("row", "col"), "dp"),
            P(("row", "col"), "dp"),
            P(("row", "col"), "dp"),
        ),
        check_vma=False,
    )
```

```python
import jax
import jax.numpy as jnp
from jax import lax
from jax.sharding import PartitionSpec as P


SPAN = 256
SEQ_LEN = 1024
ADAM_STEP = 4


PRECISE = lax.Precision.HIGHEST
SCAN_PRECISION = lax.Precision.HIGH
NORM_EPS = 1e-05
BETA_ONE = 0.9
BETA_TWO = 0.95
ADAM_EPS = 1e-08
MATRIX_RATE = 0.003
VECTOR_RATE = 0.1
WEIGHT_DECAY = 0.1


def causal_conv(values, filters):
    length = values.shape[0]
    padded = jnp.pad(values, ((3, 0), (0, 0)))
    summed = filters[4][None, :] + jnp.zeros_like(values)
    for offset in range(4):
        summed = summed + filters[offset][None, :] * padded[offset : offset + length]
    return summed


def span_scan(values, deltas, rates, key_rows, query_rows):
    length, head_count, head_width = values.shape
    states = key_rows.shape[1]
    blocks = length // SPAN
    values = values.reshape(blocks, SPAN, head_count, head_width)
    deltas = deltas.reshape(blocks, SPAN, head_count)
    key_rows = key_rows.reshape(blocks, SPAN, states)
    query_rows = query_rows.reshape(blocks, SPAN, states)
    lower = (jnp.arange(SPAN)[:, None] >= jnp.arange(SPAN)[None, :]).astype(jnp.float32)
    log_decay = jnp.einsum("qr,krh->kqh", lower, deltas * rates[None, None, :], precision=PRECISE)
    scores = jnp.einsum("kqn,krn->kqr", query_rows, key_rows, precision=SCAN_PRECISION)
    causal = jnp.arange(SPAN)[:, None] >= jnp.arange(SPAN)[None, :]
    head_decay = jnp.transpose(log_decay, (0, 2, 1))
    head_deltas = jnp.transpose(deltas, (0, 2, 1))
    spread = head_decay[:, :, :, None] - head_decay[:, :, None, :]
    decays = jnp.exp(jnp.where(causal[None, None, :, :], spread, -jnp.inf))
    mixing = scores[:, None, :, :] * decays * head_deltas[:, :, None, :]
    within = jnp.einsum("khqr,krhp->kqhp", mixing, values, precision=SCAN_PRECISION)
    to_end = jnp.exp(log_decay[:, -1:, :] - log_decay) * deltas
    produced = jnp.einsum(
        "kqn,kqh,kqhp->khnp", key_rows, to_end, values, precision=SCAN_PRECISION
    )
    factors = jnp.exp(log_decay[:, -1, :])
    carried = jnp.zeros((head_count, states, head_width), jnp.float32)
    entering = []
    for number in range(blocks):
        entering.append(carried)
        carried = carried * factors[number][:, None, None] + produced[number]
    entering = jnp.stack(entering)
    across = (
        jnp.einsum("kqn,khnp->kqhp", query_rows, entering, precision=SCAN_PRECISION)
        * jnp.exp(log_decay)[:, :, :, None]
    )
    return (within + across).reshape(length, head_count, head_width)


def mixer_sequence(gate_part, inputs, state_in, step_raw, conv_inner, conv_state, coefs):
    length = inputs.shape[0]
    head_count = coefs.shape[1]
    head_width = inputs.shape[1] // head_count
    state_size = state_in.shape[1] // 2
    conv_out = jax.nn.silu(causal_conv(inputs, conv_inner))
    state_out = jax.nn.silu(causal_conv(state_in, conv_state))
    deltas = jax.nn.softplus(step_raw + coefs[0][None, :])
    rates = -jnp.exp(coefs[1])
    shaped = conv_out.reshape(length, head_count, head_width)
    result = span_scan(shaped, deltas, rates, state_out[:, :state_size], state_out[:, state_size:])
    result = result + coefs[2][None, :, None] * shaped
    return result.reshape(length, head_count * head_width) * jax.nn.silu(gate_part)


def mixer_all(gate_part, inputs, state_in, step_raw, conv_inner, conv_state, coefs):
    seq_count = inputs.shape[0] // SEQ_LEN

    def sequence(pieces):
        return mixer_sequence(
            pieces[0], pieces[1], pieces[2], pieces[3], conv_inner, conv_state, coefs
        )

    gated = lax.map(
        sequence,
        (
            gate_part.reshape(seq_count, SEQ_LEN, -1),
            inputs.reshape(seq_count, SEQ_LEN, -1),
            state_in.reshape(seq_count, SEQ_LEN, -1),
            step_raw.reshape(seq_count, SEQ_LEN, -1),
        ),
    )
    return gated.reshape(inputs.shape[0], -1)


def adamw(weight, gradient, moment_one, moment_two, step_rate, shrink):
    new_one = BETA_ONE * moment_one + (1.0 - BETA_ONE) * gradient
    new_two = BETA_TWO * moment_two + (1.0 - BETA_TWO) * gradient * gradient
    one_hat = new_one / (1.0 - BETA_ONE**ADAM_STEP)
    two_hat = new_two / (1.0 - BETA_TWO**ADAM_STEP)
    updated = weight - step_rate * (one_hat / (jnp.sqrt(two_hat) + ADAM_EPS) + shrink * weight)
    return (updated, new_one, new_two)


def axis_bits(axis):
    return lax.axis_size(axis).bit_length() - 1


def bit_steps(*axes):
    return [(axis, k) for axis in axes for k in range(axis_bits(axis))]


def flip(x, axis, k):
    size = lax.axis_size(axis)
    return lax.ppermute(x, axis, [(j, j ^ (1 << k)) for j in range(size)])


def own_bit(axis, k):
    return (lax.axis_index(axis) >> k) & 1


def sum_bits(x, steps):
    for axis, k in steps:
        x = x + flip(x, axis, k)
    return x


def scatter_bits(x, steps):
    for axis, k in steps:
        b = own_bit(axis, k)
        keep = lax.dynamic_index_in_dim(x, b, 0, keepdims=False)
        send = lax.dynamic_index_in_dim(x, 1 - b, 0, keepdims=False)
        x = keep + flip(send, axis, k)
    return x


def gather_bits(x, steps):
    for axis, k in steps:
        other = flip(x, axis, k)
        x = jnp.where(own_bit(axis, k) == 0, jnp.stack([x, other]), jnp.stack([other, x]))
    return x


def gather_into(x, steps, names, target):
    names = list(names)
    for axis, k in steps:
        label = f"{axis}{k}"
        pos = sum(1 for n in names if target.index(n) < target.index(label))
        other = flip(x, axis, k)
        x = jnp.where(
            own_bit(axis, k) == 0,
            jnp.stack([x, other], axis=pos),
            jnp.stack([other, x], axis=pos),
        )
        names.insert(pos, label)
    return x


def bit_position(axes, step):
    axis, k = step
    below = sum(axis_bits(a) for a in axes[axes.index(axis) + 1 :])
    return below + k


def split_blocks(x, dim, axes, steps):
    total = sum(axis_bits(a) for a in axes)
    shape = x.shape[:dim] + (2,) * total + (x.shape[dim] >> total,) + x.shape[dim + 1 :]
    x = x.reshape(shape)
    front = [dim + total - 1 - bit_position(axes, s) for s in steps]
    rest = [j for j in range(len(shape)) if j not in front]
    return x.transpose(front + rest)


def pack_rows(values, width):
    flat = values.reshape(-1)
    rows = -(-flat.shape[0] // width)
    return jnp.pad(flat, (0, rows * width - flat.shape[0])).reshape(rows, width)


def two_blocks(values, first, second, width, axis):
    return jnp.concatenate(
        [
            lax.dynamic_slice_in_dim(values, first * width, width, axis),
            lax.dynamic_slice_in_dim(values, second * width, width, axis),
        ],
        axis=axis,
    )


def spread_two(values, first, second, width, total, axis):
    reps = [1] * values.ndim
    reps[axis] = total // width
    block = (jnp.arange(total) // width).reshape([-1 if k == axis else 1 for k in range(values.ndim)])
    low = jnp.tile(lax.slice_in_dim(values, 0, width, axis=axis), reps)
    high = jnp.tile(lax.slice_in_dim(values, width, 2 * width, axis=axis), reps)
    return jnp.where(block == first, low, jnp.where(block == second, high, 0.0))


def per_device(
    block_in,
    out_grad,
    norm_gain,
    first_norm_gain,
    second_norm_gain,
    input_proj,
    first_input_proj,
    second_input_proj,
    state_proj,
    first_state_proj,
    second_state_proj,
    step_proj,
    first_step_proj,
    second_step_proj,
    conv_taps,
    first_conv_taps,
    second_conv_taps,
    head_coef,
    first_head_coef,
    second_head_coef,
    gated_gain,
    first_gated_gain,
    second_gated_gain,
    output_proj,
    first_output_proj,
    second_output_proj,
):
    groups = lax.axis_size(("row", "col"))
    cols = lax.axis_size("col")
    rows = lax.axis_size("row")
    col = lax.axis_index("col")
    tok_dev = block_in.shape[0]
    model = block_in.shape[1]
    seq_tok = tok_dev * cols
    inner = gated_gain.shape[0]
    inner_dev = inner // groups
    head_total = head_coef.shape[1]
    heads_dev = head_total // groups
    head_width = inner // head_total
    n_state = state_proj.shape[1]
    n_small = n_state + step_proj.shape[1]
    rows_dev = state_proj.shape[0]
    in_rows, in_cols = input_proj.shape
    out_rows, out_cols = output_proj.shape
    low_block = col
    high_block = col + cols * (rows - 1)
    all_axes = ("dp", "row", "col")
    all_steps = bit_steps(*all_axes)
    dp_steps = bit_steps("dp")
    row_steps = bit_steps("row")
    col_steps = bit_steps("col")
    nd = len(dp_steps)
    small = jnp.concatenate([state_proj, step_proj], axis=1).astype(jnp.bfloat16)
    gather_steps = [("dp", k) for k in range(nd - 1, 0, -1)] + row_steps + [("dp", 0)]
    dp_names = [f"dp{k}" for k in range(nd - 1, -1, -1)]
    in_g = gather_into(
        input_proj.astype(jnp.bfloat16),
        gather_steps,
        ["i", "j"],
        ["row0"] + dp_names + ["i", "j"],
    ).reshape(rows, (1 << nd) * in_rows, in_cols)
    out_g = gather_into(
        output_proj.astype(jnp.bfloat16),
        gather_steps,
        ["i", "j"],
        dp_names + ["row0", "i", "j"],
    ).reshape(1 << nd, rows, out_rows, out_cols)
    x_float = block_in.astype(jnp.float32)
    inv_rms = lax.rsqrt(jnp.mean(x_float * x_float, axis=1, keepdims=True) + NORM_EPS)
    normed_in = (x_float * inv_rms * norm_gain[None, :]).astype(jnp.bfloat16)
    tokens = lax.all_gather(
        jnp.concatenate([normed_in, pack_rows(small, model)], axis=0), "col", axis=0
    )
    normed_all = tokens[:, :tok_dev].reshape(seq_tok, model)
    small_col = tokens[:, tok_dev:].reshape(cols, -1)[:, : rows_dev * n_small].reshape(-1, n_small)
    small_full = gather_bits(small_col, row_steps + dp_steps).reshape(-1, n_small)
    cotangent = lax.all_gather(out_grad, "col", axis=0, tiled=True)
    projected = jnp.einsum(
        "tD,rDj->trj", normed_all, in_g, preferred_element_type=jnp.float32
    ).reshape(seq_tok, rows * in_cols)
    small_all = jnp.dot(normed_all, small_full, preferred_element_type=jnp.float32).astype(
        jnp.bfloat16
    )
    state_all = small_all[:, :n_state]
    step_all = small_all[:, n_state:]
    local_heads = 2 * heads_dev
    local_inner = 2 * inner_dev
    paired = projected.reshape(seq_tok, local_heads, 2, head_width)
    gate_part = paired[:, :, 0, :].reshape(seq_tok, local_inner)
    inputs = paired[:, :, 1, :].reshape(seq_tok, local_inner)
    conv_inner = two_blocks(conv_taps[:, :inner], low_block, high_block, inner_dev, 1)
    conv_state = conv_taps[:, inner:]
    coefs = two_blocks(head_coef, low_block, high_block, heads_dev, 1)
    step_local = two_blocks(step_all, low_block, high_block, heads_dev, 1).astype(jnp.float32)
    gated, mixer_pull = jax.vjp(
        mixer_all,
        gate_part,
        inputs,
        state_all.astype(jnp.float32),
        step_local,
        conv_inner,
        conv_state,
        coefs,
    )
    squares = sum_bits(jnp.sum(gated * gated, axis=1), col_steps)
    gated_rms = lax.rsqrt(squares / inner + NORM_EPS)[:, None]
    gain_local = two_blocks(gated_gain, low_block, high_block, inner_dev, 0)
    normed_out = (gated * gated_rms * gain_local[None, :]).astype(jnp.bfloat16)
    mixed = lax.psum_scatter(
        jnp.einsum(
            "tri,drij->tdj",
            normed_out.reshape(seq_tok, rows, out_rows),
            out_g,
            preferred_element_type=jnp.float32,
        ).reshape(seq_tok, model),
        "col",
        scatter_dimension=0,
        tiled=True,
    )
    block_out = (x_float + mixed).astype(jnp.bfloat16)
    grad_out_local = jnp.einsum(
        "tc,td->cd", normed_out, cotangent, preferred_element_type=jnp.float32
    )
    parts = grad_out_local.reshape((rows, out_rows) + (2,) * nd + (out_cols,))
    parts = parts.transpose(tuple(range(nd + 1, 1, -1)) + (0, 1, nd + 2))
    grad_output = scatter_bits(parts, dp_steps + row_steps)
    d_normed = jnp.einsum(
        "tdj,drij->tri",
        cotangent.reshape(seq_tok, 1 << nd, out_cols),
        out_g,
        preferred_element_type=jnp.float32,
    ).reshape(seq_tok, rows * out_rows)
    gain_part = jnp.sum(d_normed * gated * gated_rms, axis=0)
    scaled = d_normed * gain_local[None, :]
    cross = sum_bits(jnp.sum(scaled * gated, axis=1), col_steps)
    d_gated = gated_rms * scaled - gated * gated_rms**3 * (cross / inner)[:, None]
    d_gate, d_inputs, d_state, d_step, d_conv_inner, d_conv_state, d_coefs = mixer_pull(
        d_gated
    )
    d_projected = (
        jnp.stack(
            [
                d_gate.reshape(seq_tok, local_heads, head_width),
                d_inputs.reshape(seq_tok, local_heads, head_width),
            ],
            axis=2,
        )
        .reshape(seq_tok, 2 * local_inner)
        .astype(jnp.bfloat16)
    )
    grad_in_local = jnp.einsum(
        "td,tc->dc", normed_all, d_projected, preferred_element_type=jnp.float32
    )
    step_spread = spread_two(d_step, low_block, high_block, heads_dev, head_total, 1)
    back_all = lax.psum_scatter(
        jnp.concatenate(
            [
                jnp.einsum(
                    "trj,rDj->tD",
                    d_projected.reshape(seq_tok, rows, in_cols),
                    in_g,
                    preferred_element_type=jnp.float32,
                ),
                d_state,
                step_spread,
            ],
            axis=1,
        ),
        "col",
        scatter_dimension=0,
        tiled=True,
    )
    d_normed_in = back_all[:, :model]
    small_back = back_all[:, model:].astype(jnp.bfloat16)
    d_normed_in = d_normed_in + jnp.einsum(
        "tc,dc->td", small_back, small_full, preferred_element_type=jnp.float32
    )
    grad_small_part = jnp.einsum(
        "td,tc->dc", normed_in, small_back, preferred_element_type=jnp.float32
    )
    parts = grad_in_local.reshape((2,) * nd + (in_rows, rows, in_cols))
    parts = parts.transpose(tuple(range(nd - 1, -1, -1)) + (nd + 1, nd, nd + 2))
    half = in_cols // 2
    first_half = scatter_bits(parts[..., :half], dp_steps + row_steps)
    swapped = jnp.moveaxis(parts[..., half:], nd, 1)
    second_half = scatter_bits(swapped, dp_steps[:1] + row_steps + dp_steps[1:])
    grad_input = jnp.concatenate([first_half, second_half], axis=1)
    scaled_in = d_normed_in * norm_gain[None, :]
    norm_part = jnp.sum(d_normed_in * x_float * inv_rms, axis=0)
    input_grad = (
        out_grad.astype(jnp.float32)
        + inv_rms * scaled_in
        - x_float * inv_rms**3 * jnp.mean(scaled_in * x_float, axis=1, keepdims=True)
    )
    gated_spread = spread_two(gain_part, low_block, high_block, inner_dev, inner, 0)
    conv_front = spread_two(d_conv_inner, low_block, high_block, inner_dev, inner, 1)
    conv_spread = jnp.concatenate([conv_front, d_conv_state], axis=1)
    coef_spread = spread_two(d_coefs, low_block, high_block, heads_dev, head_total, 1)
    pieces = (norm_part, gated_spread, conv_spread, coef_spread)
    offsets = [0]
    for piece in pieces:
        offsets.append(offsets[-1] + piece.size)
    packed = pack_rows(jnp.concatenate([piece.reshape(-1) for piece in pieces]), n_small)
    summed_flat = sum_bits(packed, all_steps).reshape(-1)
    grad_small = scatter_bits(split_blocks(grad_small_part, 0, all_axes, all_steps), all_steps)
    grad_norm, grad_gated, grad_conv, grad_coef = (
        summed_flat[offsets[k] : offsets[k + 1]].reshape(piece.shape)
        for k, piece in enumerate(pieces)
    )
    grad_state = grad_small[:, :n_state]
    grad_step = grad_small[:, n_state:]
    n_norm, f_norm, s_norm = adamw(
        norm_gain, grad_norm, first_norm_gain, second_norm_gain, VECTOR_RATE, 0.0
    )
    n_input, f_input, s_input = adamw(
        input_proj, grad_input, first_input_proj, second_input_proj, MATRIX_RATE, WEIGHT_DECAY
    )
    n_state, f_state, s_state = adamw(
        state_proj, grad_state, first_state_proj, second_state_proj, MATRIX_RATE, WEIGHT_DECAY
    )
    n_step, f_step, s_step = adamw(
        step_proj, grad_step, first_step_proj, second_step_proj, MATRIX_RATE, WEIGHT_DECAY
    )
    n_conv, f_conv, s_conv = adamw(
        conv_taps, grad_conv, first_conv_taps, second_conv_taps, VECTOR_RATE, 0.0
    )
    n_head, f_head, s_head = adamw(
        head_coef, grad_coef, first_head_coef, second_head_coef, VECTOR_RATE, 0.0
    )
    n_gated, f_gated, s_gated = adamw(
        gated_gain, grad_gated, first_gated_gain, second_gated_gain, VECTOR_RATE, 0.0
    )
    n_output, f_output, s_output = adamw(
        output_proj, grad_output, first_output_proj, second_output_proj, MATRIX_RATE, WEIGHT_DECAY
    )
    return (
        block_out,
        input_grad,
        grad_norm,
        grad_input,
        grad_state,
        grad_step,
        grad_conv,
        grad_coef,
        grad_gated,
        grad_output,
        n_norm,
        f_norm,
        s_norm,
        n_input,
        f_input,
        s_input,
        n_state,
        f_state,
        s_state,
        n_step,
        f_step,
        s_step,
        n_conv,
        f_conv,
        s_conv,
        n_head,
        f_head,
        s_head,
        n_gated,
        f_gated,
        s_gated,
        n_output,
        f_output,
        s_output,
    )


def solution(mesh):
    return jax.shard_map(
        per_device,
        mesh=mesh,
        in_specs=(
            P(("dp", "row", "col"), None),
            P(("dp", "row", "col"), None),
            P(),
            P(),
            P(),
            P("dp", ("row", "col")),
            P("dp", ("row", "col")),
            P("dp", ("row", "col")),
            P(("dp", "row", "col"), None),
            P(("dp", "row", "col"), None),
            P(("dp", "row", "col"), None),
            P(("dp", "row", "col"), None),
            P(("dp", "row", "col"), None),
            P(("dp", "row", "col"), None),
            P(),
            P(),
            P(),
            P(),
            P(),
            P(),
            P(),
            P(),
            P(),
            P(("row", "col"), "dp"),
            P(("row", "col"), "dp"),
            P(("row", "col"), "dp"),
        ),
        out_specs=(
            P(("dp", "row", "col"), None),
            P(("dp", "row", "col"), None),
            P(),
            P("dp", ("row", "col")),
            P(("dp", "row", "col"), None),
            P(("dp", "row", "col"), None),
            P(),
            P(),
            P(),
            P(("row", "col"), "dp"),
            P(),
            P(),
            P(),
            P("dp", ("row", "col")),
            P("dp", ("row", "col")),
            P("dp", ("row", "col")),
            P(("dp", "row", "col"), None),
            P(("dp", "row", "col"), None),
            P(("dp", "row", "col"), None),
            P(("dp", "row", "col"), None),
            P(("dp", "row", "col"), None),
            P(("dp", "row", "col"), None),
            P(),
            P(),
            P(),
            P(),
            P(),
            P(),
            P(),
            P(),
            P(),
            P(("row", "col"), "dp"),
            P(("row", "col"), "dp"),
            P(("row", "col"), "dp"),
        ),
        check_vma=False,
    )
```

```python
import jax
import jax.numpy as jnp
from jax import lax
from jax.sharding import PartitionSpec as P


SPAN = 256
SEQ_LEN = 1024
ADAM_STEP = 4


PRECISE = lax.Precision.HIGHEST
SCAN_PRECISION = lax.Precision.HIGH
NORM_EPS = 1e-05
BETA_ONE = 0.9
BETA_TWO = 0.95
ADAM_EPS = 1e-08
MATRIX_RATE = 0.003
VECTOR_RATE = 0.1
WEIGHT_DECAY = 0.1


def causal_conv(values, filters):
    length = values.shape[0]
    padded = jnp.pad(values, ((3, 0), (0, 0)))
    summed = filters[4][None, :] + jnp.zeros_like(values)
    for offset in range(4):
        summed = summed + filters[offset][None, :] * padded[offset : offset + length]
    return summed


def span_scan(values, deltas, rates, key_rows, query_rows):
    length, head_count, head_width = values.shape
    states = key_rows.shape[1]
    blocks = length // SPAN
    values = values.reshape(blocks, SPAN, head_count, head_width)
    deltas = deltas.reshape(blocks, SPAN, head_count)
    key_rows = key_rows.reshape(blocks, SPAN, states)
    query_rows = query_rows.reshape(blocks, SPAN, states)
    lower = (jnp.arange(SPAN)[:, None] >= jnp.arange(SPAN)[None, :]).astype(jnp.float32)
    log_decay = jnp.einsum("qr,krh->kqh", lower, deltas * rates[None, None, :], precision=PRECISE)
    scores = jnp.einsum("kqn,krn->kqr", query_rows, key_rows, precision=SCAN_PRECISION)
    causal = jnp.arange(SPAN)[:, None] >= jnp.arange(SPAN)[None, :]
    head_decay = jnp.transpose(log_decay, (0, 2, 1))
    head_deltas = jnp.transpose(deltas, (0, 2, 1))
    spread = head_decay[:, :, :, None] - head_decay[:, :, None, :]
    decays = jnp.exp(jnp.where(causal[None, None, :, :], spread, -jnp.inf))
    mixing = scores[:, None, :, :] * decays * head_deltas[:, :, None, :]
    within = jnp.einsum("khqr,krhp->kqhp", mixing, values, precision=SCAN_PRECISION)
    to_end = jnp.exp(log_decay[:, -1:, :] - log_decay) * deltas
    produced = jnp.einsum(
        "kqn,kqh,kqhp->khnp", key_rows, to_end, values, precision=SCAN_PRECISION
    )
    factors = jnp.exp(log_decay[:, -1, :])
    carried = jnp.zeros((head_count, states, head_width), jnp.float32)
    entering = []
    for number in range(blocks):
        entering.append(carried)
        carried = carried * factors[number][:, None, None] + produced[number]
    entering = jnp.stack(entering)
    across = (
        jnp.einsum("kqn,khnp->kqhp", query_rows, entering, precision=SCAN_PRECISION)
        * jnp.exp(log_decay)[:, :, :, None]
    )
    return (within + across).reshape(length, head_count, head_width)


def mixer_sequence(gate_part, inputs, state_in, step_raw, conv_inner, conv_state, coefs):
    length = inputs.shape[0]
    head_count = coefs.shape[1]
    head_width = inputs.shape[1] // head_count
    state_size = state_in.shape[1] // 2
    conv_out = jax.nn.silu(causal_conv(inputs, conv_inner))
    state_out = jax.nn.silu(causal_conv(state_in, conv_state))
    deltas = jax.nn.softplus(step_raw + coefs[0][None, :])
    rates = -jnp.exp(coefs[1])
    shaped = conv_out.reshape(length, head_count, head_width)
    result = span_scan(shaped, deltas, rates, state_out[:, :state_size], state_out[:, state_size:])
    result = result + coefs[2][None, :, None] * shaped
    return result.reshape(length, head_count * head_width) * jax.nn.silu(gate_part)


def mixer_all(gate_part, inputs, state_in, step_raw, conv_inner, conv_state, coefs):
    seq_count = inputs.shape[0] // SEQ_LEN

    def sequence(pieces):
        return mixer_sequence(
            pieces[0], pieces[1], pieces[2], pieces[3], conv_inner, conv_state, coefs
        )

    gated = lax.map(
        sequence,
        (
            gate_part.reshape(seq_count, SEQ_LEN, -1),
            inputs.reshape(seq_count, SEQ_LEN, -1),
            state_in.reshape(seq_count, SEQ_LEN, -1),
            step_raw.reshape(seq_count, SEQ_LEN, -1),
        ),
    )
    return gated.reshape(inputs.shape[0], -1)


def adamw(weight, gradient, moment_one, moment_two, step_rate, shrink):
    new_one = BETA_ONE * moment_one + (1.0 - BETA_ONE) * gradient
    new_two = BETA_TWO * moment_two + (1.0 - BETA_TWO) * gradient * gradient
    one_hat = new_one / (1.0 - BETA_ONE**ADAM_STEP)
    two_hat = new_two / (1.0 - BETA_TWO**ADAM_STEP)
    updated = weight - step_rate * (one_hat / (jnp.sqrt(two_hat) + ADAM_EPS) + shrink * weight)
    return (updated, new_one, new_two)


def axis_bits(axis):
    return lax.axis_size(axis).bit_length() - 1


def bit_steps(*axes):
    return [(axis, k) for axis in axes for k in range(axis_bits(axis))]


def flip(x, axis, k):
    size = lax.axis_size(axis)
    return lax.ppermute(x, axis, [(j, j ^ (1 << k)) for j in range(size)])


def own_bit(axis, k):
    return (lax.axis_index(axis) >> k) & 1


def sum_bits(x, steps):
    for axis, k in steps:
        x = x + flip(x, axis, k)
    return x


def scatter_bits(x, steps):
    for axis, k in steps:
        b = own_bit(axis, k)
        keep = lax.dynamic_index_in_dim(x, b, 0, keepdims=False)
        send = lax.dynamic_index_in_dim(x, 1 - b, 0, keepdims=False)
        x = keep + flip(send, axis, k)
    return x


def scatter_sum_bits(x, extra, steps):
    for axis, k in steps:
        b = own_bit(axis, k)
        keep = lax.dynamic_index_in_dim(x, b, 0, keepdims=False)
        send = lax.dynamic_index_in_dim(x, 1 - b, 0, keepdims=False)
        flat = send.reshape(-1, extra.shape[1])
        got = flip(jnp.concatenate([flat, extra], axis=0), axis, k)
        x = keep + got[: flat.shape[0]].reshape(send.shape)
        extra = extra + got[flat.shape[0] :]
    return x, extra


def gather_bits(x, steps):
    for axis, k in steps:
        other = flip(x, axis, k)
        x = jnp.where(own_bit(axis, k) == 0, jnp.stack([x, other]), jnp.stack([other, x]))
    return x


def gather_into(x, steps, names, target):
    names = list(names)
    for axis, k in steps:
        label = f"{axis}{k}"
        pos = sum(1 for n in names if target.index(n) < target.index(label))
        other = flip(x, axis, k)
        x = jnp.where(
            own_bit(axis, k) == 0,
            jnp.stack([x, other], axis=pos),
            jnp.stack([other, x], axis=pos),
        )
        names.insert(pos, label)
    return x


def bit_position(axes, step):
    axis, k = step
    below = sum(axis_bits(a) for a in axes[axes.index(axis) + 1 :])
    return below + k


def split_blocks(x, dim, axes, steps):
    total = sum(axis_bits(a) for a in axes)
    shape = x.shape[:dim] + (2,) * total + (x.shape[dim] >> total,) + x.shape[dim + 1 :]
    x = x.reshape(shape)
    front = [dim + total - 1 - bit_position(axes, s) for s in steps]
    rest = [j for j in range(len(shape)) if j not in front]
    return x.transpose(front + rest)


def pack_rows(values, width):
    flat = values.reshape(-1)
    rows = -(-flat.shape[0] // width)
    return jnp.pad(flat, (0, rows * width - flat.shape[0])).reshape(rows, width)


def two_blocks(values, first, second, width, axis):
    return jnp.concatenate(
        [
            lax.dynamic_slice_in_dim(values, first * width, width, axis),
            lax.dynamic_slice_in_dim(values, second * width, width, axis),
        ],
        axis=axis,
    )


def spread_two(values, first, second, width, total, axis):
    reps = [1] * values.ndim
    reps[axis] = total // width
    block = (jnp.arange(total) // width).reshape([-1 if k == axis else 1 for k in range(values.ndim)])
    low = jnp.tile(lax.slice_in_dim(values, 0, width, axis=axis), reps)
    high = jnp.tile(lax.slice_in_dim(values, width, 2 * width, axis=axis), reps)
    return jnp.where(block == first, low, jnp.where(block == second, high, 0.0))


def per_device(
    block_in,
    out_grad,
    norm_gain,
    first_norm_gain,
    second_norm_gain,
    input_proj,
    first_input_proj,
    second_input_proj,
    state_proj,
    first_state_proj,
    second_state_proj,
    step_proj,
    first_step_proj,
    second_step_proj,
    conv_taps,
    first_conv_taps,
    second_conv_taps,
    head_coef,
    first_head_coef,
    second_head_coef,
    gated_gain,
    first_gated_gain,
    second_gated_gain,
    output_proj,
    first_output_proj,
    second_output_proj,
):
    groups = lax.axis_size(("row", "col"))
    cols = lax.axis_size("col")
    rows = lax.axis_size("row")
    col = lax.axis_index("col")
    tok_dev = block_in.shape[0]
    model = block_in.shape[1]
    seq_tok = tok_dev * cols
    inner = gated_gain.shape[0]
    inner_dev = inner // groups
    head_total = head_coef.shape[1]
    heads_dev = head_total // groups
    head_width = inner // head_total
    n_state = state_proj.shape[1]
    n_small = n_state + step_proj.shape[1]
    rows_dev = state_proj.shape[0]
    in_rows, in_cols = input_proj.shape
    out_rows, out_cols = output_proj.shape
    low_block = col
    high_block = col + cols * (rows - 1)
    all_axes = ("dp", "row", "col")
    all_steps = bit_steps(*all_axes)
    dp_steps = bit_steps("dp")
    row_steps = bit_steps("row")
    col_steps = bit_steps("col")
    nd = len(dp_steps)
    small = jnp.concatenate([state_proj, step_proj], axis=1).astype(jnp.bfloat16)
    gather_steps = [("dp", k) for k in range(nd - 1, 0, -1)] + row_steps + [("dp", 0)]
    dp_names = [f"dp{k}" for k in range(nd - 1, -1, -1)]
    in_g = gather_into(
        input_proj.astype(jnp.bfloat16),
        gather_steps,
        ["i", "j"],
        ["row0"] + dp_names + ["i", "j"],
    ).reshape(rows, (1 << nd) * in_rows, in_cols)
    out_g = gather_into(
        output_proj.astype(jnp.bfloat16),
        gather_steps,
        ["i", "j"],
        dp_names + ["row0", "i", "j"],
    ).reshape(1 << nd, rows, out_rows, out_cols)
    x_float = block_in.astype(jnp.float32)
    inv_rms = lax.rsqrt(jnp.mean(x_float * x_float, axis=1, keepdims=True) + NORM_EPS)
    normed_in = (x_float * inv_rms * norm_gain[None, :]).astype(jnp.bfloat16)
    tokens = lax.all_gather(
        jnp.concatenate([normed_in, pack_rows(small, model)], axis=0), "col", axis=0
    )
    normed_all = tokens[:, :tok_dev].reshape(seq_tok, model)
    small_col = tokens[:, tok_dev:].reshape(cols, -1)[:, : rows_dev * n_small].reshape(-1, n_small)
    small_full = gather_bits(small_col, row_steps + dp_steps).reshape(-1, n_small)
    cotangent = lax.all_gather(out_grad, "col", axis=0, tiled=True)
    projected = jnp.einsum(
        "tD,rDj->trj", normed_all, in_g, preferred_element_type=jnp.float32
    ).reshape(seq_tok, rows * in_cols)
    small_all = jnp.dot(normed_all, small_full, preferred_element_type=jnp.float32).astype(
        jnp.bfloat16
    )
    state_all = small_all[:, :n_state]
    step_all = small_all[:, n_state:]
    local_heads = 2 * heads_dev
    local_inner = 2 * inner_dev
    paired = projected.reshape(seq_tok, local_heads, 2, head_width)
    gate_part = paired[:, :, 0, :].reshape(seq_tok, local_inner)
    inputs = paired[:, :, 1, :].reshape(seq_tok, local_inner)
    conv_inner = two_blocks(conv_taps[:, :inner], low_block, high_block, inner_dev, 1)
    conv_state = conv_taps[:, inner:]
    coefs = two_blocks(head_coef, low_block, high_block, heads_dev, 1)
    step_local = two_blocks(step_all, low_block, high_block, heads_dev, 1).astype(jnp.float32)
    gated, mixer_pull = jax.vjp(
        mixer_all,
        gate_part,
        inputs,
        state_all.astype(jnp.float32),
        step_local,
        conv_inner,
        conv_state,
        coefs,
    )
    squares = sum_bits(jnp.sum(gated * gated, axis=1), col_steps)
    gated_rms = lax.rsqrt(squares / inner + NORM_EPS)[:, None]
    gain_local = two_blocks(gated_gain, low_block, high_block, inner_dev, 0)
    normed_out = (gated * gated_rms * gain_local[None, :]).astype(jnp.bfloat16)
    mixed = lax.psum_scatter(
        jnp.einsum(
            "tri,drij->tdj",
            normed_out.reshape(seq_tok, rows, out_rows),
            out_g,
            preferred_element_type=jnp.float32,
        ).reshape(seq_tok, model),
        "col",
        scatter_dimension=0,
        tiled=True,
    )
    block_out = (x_float + mixed).astype(jnp.bfloat16)
    grad_out_local = jnp.einsum(
        "tc,td->cd", normed_out, cotangent, preferred_element_type=jnp.float32
    )
    parts = grad_out_local.reshape((rows, out_rows) + (2,) * nd + (out_cols,))
    parts = parts.transpose(tuple(range(nd + 1, 1, -1)) + (0, 1, nd + 2))
    grad_output = scatter_bits(parts, dp_steps + row_steps)
    d_normed = jnp.einsum(
        "tdj,drij->tri",
        cotangent.reshape(seq_tok, 1 << nd, out_cols),
        out_g,
        preferred_element_type=jnp.float32,
    ).reshape(seq_tok, rows * out_rows)
    gain_part = jnp.sum(d_normed * gated * gated_rms, axis=0)
    scaled = d_normed * gain_local[None, :]
    cross = sum_bits(jnp.sum(scaled * gated, axis=1), col_steps)
    d_gated = gated_rms * scaled - gated * gated_rms**3 * (cross / inner)[:, None]
    d_gate, d_inputs, d_state, d_step, d_conv_inner, d_conv_state, d_coefs = mixer_pull(
        d_gated
    )
    d_projected = (
        jnp.stack(
            [
                d_gate.reshape(seq_tok, local_heads, head_width),
                d_inputs.reshape(seq_tok, local_heads, head_width),
            ],
            axis=2,
        )
        .reshape(seq_tok, 2 * local_inner)
        .astype(jnp.bfloat16)
    )
    grad_in_local = jnp.einsum(
        "td,tc->dc", normed_all, d_projected, preferred_element_type=jnp.float32
    )
    step_spread = spread_two(d_step, low_block, high_block, heads_dev, head_total, 1)
    back_all = lax.psum_scatter(
        jnp.concatenate(
            [
                jnp.einsum(
                    "trj,rDj->tD",
                    d_projected.reshape(seq_tok, rows, in_cols),
                    in_g,
                    preferred_element_type=jnp.float32,
                ),
                d_state,
                step_spread,
            ],
            axis=1,
        ),
        "col",
        scatter_dimension=0,
        tiled=True,
    )
    d_normed_in = back_all[:, :model]
    small_back = back_all[:, model:].astype(jnp.bfloat16)
    d_normed_in = d_normed_in + jnp.einsum(
        "tc,dc->td", small_back, small_full, preferred_element_type=jnp.float32
    )
    grad_small_part = jnp.einsum(
        "td,tc->dc", normed_in, small_back, preferred_element_type=jnp.float32
    )
    parts = grad_in_local.reshape((2,) * nd + (in_rows, rows, in_cols))
    parts = parts.transpose(tuple(range(nd - 1, -1, -1)) + (nd + 1, nd, nd + 2))
    half = in_cols // 2
    first_half = scatter_bits(parts[..., :half], dp_steps + row_steps)
    swapped = jnp.moveaxis(parts[..., half:], nd, 1)
    second_half = scatter_bits(swapped, dp_steps[:1] + row_steps + dp_steps[1:])
    grad_input = jnp.concatenate([first_half, second_half], axis=1)
    scaled_in = d_normed_in * norm_gain[None, :]
    norm_part = jnp.sum(d_normed_in * x_float * inv_rms, axis=0)
    input_grad = (
        out_grad.astype(jnp.float32)
        + inv_rms * scaled_in
        - x_float * inv_rms**3 * jnp.mean(scaled_in * x_float, axis=1, keepdims=True)
    )
    gated_spread = spread_two(gain_part, low_block, high_block, inner_dev, inner, 0)
    conv_front = spread_two(d_conv_inner, low_block, high_block, inner_dev, inner, 1)
    conv_spread = jnp.concatenate([conv_front, d_conv_state], axis=1)
    coef_spread = spread_two(d_coefs, low_block, high_block, heads_dev, head_total, 1)
    pieces = (norm_part, gated_spread, conv_spread, coef_spread)
    offsets = [0]
    for piece in pieces:
        offsets.append(offsets[-1] + piece.size)
    packed = pack_rows(jnp.concatenate([piece.reshape(-1) for piece in pieces]), n_small)
    grad_small, summed = scatter_sum_bits(
        split_blocks(grad_small_part, 0, all_axes, all_steps), packed, all_steps
    )
    summed_flat = summed.reshape(-1)
    grad_norm, grad_gated, grad_conv, grad_coef = (
        summed_flat[offsets[k] : offsets[k + 1]].reshape(piece.shape)
        for k, piece in enumerate(pieces)
    )
    grad_state = grad_small[:, :n_state]
    grad_step = grad_small[:, n_state:]
    n_norm, f_norm, s_norm = adamw(
        norm_gain, grad_norm, first_norm_gain, second_norm_gain, VECTOR_RATE, 0.0
    )
    n_input, f_input, s_input = adamw(
        input_proj, grad_input, first_input_proj, second_input_proj, MATRIX_RATE, WEIGHT_DECAY
    )
    n_state, f_state, s_state = adamw(
        state_proj, grad_state, first_state_proj, second_state_proj, MATRIX_RATE, WEIGHT_DECAY
    )
    n_step, f_step, s_step = adamw(
        step_proj, grad_step, first_step_proj, second_step_proj, MATRIX_RATE, WEIGHT_DECAY
    )
    n_conv, f_conv, s_conv = adamw(
        conv_taps, grad_conv, first_conv_taps, second_conv_taps, VECTOR_RATE, 0.0
    )
    n_head, f_head, s_head = adamw(
        head_coef, grad_coef, first_head_coef, second_head_coef, VECTOR_RATE, 0.0
    )
    n_gated, f_gated, s_gated = adamw(
        gated_gain, grad_gated, first_gated_gain, second_gated_gain, VECTOR_RATE, 0.0
    )
    n_output, f_output, s_output = adamw(
        output_proj, grad_output, first_output_proj, second_output_proj, MATRIX_RATE, WEIGHT_DECAY
    )
    return (
        block_out,
        input_grad,
        grad_norm,
        grad_input,
        grad_state,
        grad_step,
        grad_conv,
        grad_coef,
        grad_gated,
        grad_output,
        n_norm,
        f_norm,
        s_norm,
        n_input,
        f_input,
        s_input,
        n_state,
        f_state,
        s_state,
        n_step,
        f_step,
        s_step,
        n_conv,
        f_conv,
        s_conv,
        n_head,
        f_head,
        s_head,
        n_gated,
        f_gated,
        s_gated,
        n_output,
        f_output,
        s_output,
    )


def solution(mesh):
    return jax.shard_map(
        per_device,
        mesh=mesh,
        in_specs=(
            P(("dp", "row", "col"), None),
            P(("dp", "row", "col"), None),
            P(),
            P(),
            P(),
            P("dp", ("row", "col")),
            P("dp", ("row", "col")),
            P("dp", ("row", "col")),
            P(("dp", "row", "col"), None),
            P(("dp", "row", "col"), None),
            P(("dp", "row", "col"), None),
            P(("dp", "row", "col"), None),
            P(("dp", "row", "col"), None),
            P(("dp", "row", "col"), None),
            P(),
            P(),
            P(),
            P(),
            P(),
            P(),
            P(),
            P(),
            P(),
            P(("row", "col"), "dp"),
            P(("row", "col"), "dp"),
            P(("row", "col"), "dp"),
        ),
        out_specs=(
            P(("dp", "row", "col"), None),
            P(("dp", "row", "col"), None),
            P(),
            P("dp", ("row", "col")),
            P(("dp", "row", "col"), None),
            P(("dp", "row", "col"), None),
            P(),
            P(),
            P(),
            P(("row", "col"), "dp"),
            P(),
            P(),
            P(),
            P("dp", ("row", "col")),
            P("dp", ("row", "col")),
            P("dp", ("row", "col")),
            P(("dp", "row", "col"), None),
            P(("dp", "row", "col"), None),
            P(("dp", "row", "col"), None),
            P(("dp", "row", "col"), None),
            P(("dp", "row", "col"), None),
            P(("dp", "row", "col"), None),
            P(),
            P(),
            P(),
            P(),
            P(),
            P(),
            P(),
            P(),
            P(),
            P(("row", "col"), "dp"),
            P(("row", "col"), "dp"),
            P(("row", "col"), "dp"),
        ),
        check_vma=False,
    )
```
